128 devices in a mesh: src: 16 (over y_lo, z, core), tgt: 8 (over y_hi, x).
Axes of the slice: x: 4, y: 4 (y_hi: 2, y_lo: 2; y = y_hi * 2 + y_lo), z: 4, core: 2. Of those that a mesh axis runs over, the one named last changes fastest.
Arguments:
- src_emb: bfloat16 [16384, 768], P(('src', 'tgt')), may hold values from -0.05119037 to 0.05119037
- right_sentence_vectors: bfloat16 [8192, 768], P(('tgt', 'src')), may hold values from -0.05119037 to 0.05119037
- src_mass: float32 [16384], P('src'), may hold values from 0.25 to 4
- tgt_mass: float32 [8192], P('tgt'), may hold values from 0.5 to 8
Outputs:
- grad_src: float32 [16384, 768], P(('src', 'tgt'))
- grad_tgt: float32 [8192, 768], P(('tgt', 'src'))
The draws below stay inside these ranges and needn't reach their ends.
All inputs are finite; a program needn't handle non-finite values.
Results may differ from the reference program's by a relative error of at most 0.00045.
Values may be sent and summed in bfloat16 or wider, within the bound.
No kernel may reach another device: no remote copies, remote signals or barrier semaphores. Data moves between devices by JAX's collectives and lax.ppermute only.
A program may use at most 64 MiB of HBM per device.

```python
import math
import jax
import jax.numpy as jnp
from jax import lax

D = 768
ITERS = 4
NS = 16384
NT = 8192


def shared_direction(key):
    amplitude = (0.7 / D) ** 0.5
    signs = jax.random.bernoulli(jax.random.fold_in(key, 7), 0.5, (D,))
    magnitude = amplitude * jnp.ones((D,), jnp.float32)
    return jnp.where(signs, magnitude, -magnitude).astype(jnp.float32)


def placed_rows(key, count, salt):
    direction = shared_direction(key)
    position = (jnp.arange(count, dtype=jnp.float32) + 0.5) / count * 2.0 - 1.0
    jitter = jax.random.uniform(jax.random.fold_in(key, salt), (count,), jnp.float32, -0.2, 0.2)
    level = 0.8 * position + jitter
    noise = jax.random.uniform(jax.random.fold_in(key, salt + 1), (count, D), jnp.float32, -0.02, 0.02)
    return level[:, None] * direction[None, :] + noise


def draw_src_emb(key, part):
    return placed_rows(key, NS, 11).astype(jnp.bfloat16)


def draw_right_sentence_vectors(key, part):
    return placed_rows(key, NT, 23).astype(jnp.bfloat16)


def level_of(rng, extent, split, smallest, largest):
    factor_of, own = 1.0, jax.random.fold_in(rng, 6)
    for axis_at, shards_of in split:
        steps = jnp.exp(jax.random.uniform(jax.random.fold_in(own, axis_at), (shards_of,), jnp.float32, smallest / len(split), largest / len(split)))
        factor_of = factor_of * jnp.repeat(steps, extent[axis_at] // shards_of).reshape([-1 if axis == axis_at else 1 for axis in range(len(extent))])
    return factor_of


def setup_inputs(seed: int = 0) -> dict:
    key_of = jax.random.split(jax.random.key(seed), 5)
    src_emb = draw_src_emb(jax.random.fold_in(key_of[4], 71), 0)
    right_sentence_vectors = draw_right_sentence_vectors(jax.random.fold_in(key_of[4], 71), 0)
    src_mass = jnp.clip(jnp.exp(math.log(4.0) - 2.7725887 * jax.random.uniform(key_of[2], (NS,), jnp.float32) ** level_of(key_of[2], (NS,), ((0, 16),), -0.2, 0.2)), 0.25, 4.0)
    tgt_mass = jnp.clip(jnp.exp(math.log(8.0) - 2.7725887 * jax.random.uniform(key_of[3], (NT,), jnp.float32) ** level_of(key_of[3], (NT,), ((0, 8),), -0.2, 0.2)), 0.5, 8.0)
    return dict(src_emb=src_emb, right_sentence_vectors=right_sentence_vectors, src_mass=src_mass, tgt_mass=tgt_mass)


regularizer_epsilon = 0.05
highest = lax.Precision.HIGHEST


def make_tile(tile_window, right_sentence_vectors):
    kernel_grid = jnp.dot(tile_window, right_sentence_vectors.T, preferred_element_type=jnp.float32) / regularizer_epsilon
    kernel = lax.optimization_barrier(jnp.exp(kernel_grid).astype(jnp.bfloat16))
    return kernel_grid, kernel


def reference(src_emb, right_sentence_vectors, src_mass, tgt_mass):
    all_rows = src_emb.shape[0]
    block_rows = math.gcd(all_rows, 2048)
    block_count = all_rows // block_rows
    blocks = src_emb.reshape(block_count, block_rows, src_emb.shape[1])
    zeros_tgt = jnp.zeros(right_sentence_vectors.shape[0], jnp.float32)

    def row_pass(vector):
        def per_block(tile_window):
            kernel_grid, kernel = make_tile(tile_window, right_sentence_vectors)
            return jnp.dot(kernel, vector, precision=highest, preferred_element_type=jnp.float32)
        return lax.map(per_block, blocks).reshape(all_rows)

    def col_pass(vector):
        pieces = vector.reshape(block_count, block_rows)

        def per_block(running, member):
            kernel_grid, kernel = make_tile(member[0], right_sentence_vectors)
            return running + jnp.dot(member[1], kernel, precision=highest, preferred_element_type=jnp.float32), None
        result, unused = lax.scan(per_block, zeros_tgt, (blocks, pieces))
        return result

    vector = jnp.ones(right_sentence_vectors.shape[0], jnp.float32)
    old_saved, row_saved, src_saved, col_saved, tgt_saved = [], [], [], [], []
    for iteration in range(ITERS):
        old_saved.append(vector)
        row_total = row_pass(vector)
        src_scale = src_mass / row_total
        col_total = col_pass(src_scale)
        vector = tgt_mass / col_total
        row_saved.append(row_total)
        src_saved.append(src_scale)
        col_saved.append(col_total)
        tgt_saved.append(vector)
    last_src = src_saved[-1]
    last_tgt = tgt_saved[-1]

    def first_block(running, member):
        kernel_grid, kernel = make_tile(member[0], right_sentence_vectors)
        weighted = kernel * kernel_grid
        row_part = jnp.dot(weighted, last_tgt, precision=highest, preferred_element_type=jnp.float32)
        col_part = jnp.dot(member[1], weighted, precision=highest, preferred_element_type=jnp.float32)
        return running + col_part, row_part

    tgt_adj, row_parts = lax.scan(first_block, zeros_tgt, (blocks, last_src.reshape(block_count, block_rows)))
    src_adj = row_parts.reshape(all_rows)
    row_bars = [None] * ITERS
    col_bars = [None] * ITERS
    for iteration in reversed(range(ITERS)):
        col_bar = -tgt_adj * tgt_saved[iteration] / col_saved[iteration]
        back = row_pass(col_bar)
        if iteration == ITERS - 1:
            back = back + src_adj
        row_bar = -back * src_saved[iteration] / row_saved[iteration]
        if iteration > 0:
            tgt_adj = col_pass(row_bar)
        row_bars[iteration] = row_bar
        col_bars[iteration] = col_bar
    left = jnp.stack(row_bars + src_saved, axis=1)
    right = jnp.stack(old_saved + col_bars, axis=1)

    def grad_block(running, member):
        tile_window, left_rows, scale_rows = member
        kernel_grid, kernel = make_tile(tile_window, right_sentence_vectors)
        lowrank = jnp.dot(left_rows, right.T, precision=highest, preferred_element_type=jnp.float32)
        cross_term_grid = (kernel * (scale_rows[:, None] * last_tgt[None, :] * (1.0 + kernel_grid) + lowrank)).astype(jnp.bfloat16)
        left_share_piece = jnp.dot(cross_term_grid, right_sentence_vectors, preferred_element_type=jnp.float32) / regularizer_epsilon
        right_share_piece = lax.dot_general(cross_term_grid, tile_window, (((0,), (0,)), ((), ())), preferred_element_type=jnp.float32) / regularizer_epsilon
        return running + right_share_piece, left_share_piece

    zeros_grad = jnp.zeros(right_sentence_vectors.shape, jnp.float32)
    members = (blocks, left.reshape(block_count, block_rows, left.shape[1]), last_src.reshape(block_count, block_rows))
    grad_tgt, src_parts = lax.scan(grad_block, zeros_grad, members)
    return src_parts.reshape(all_rows, src_emb.shape[1]), grad_tgt
```

```python
import jax
import jax.numpy as jnp
from jax import lax
from jax.sharding import PartitionSpec as P

ITERS = 4


regularizer_epsilon = 0.05
highest = lax.Precision.HIGHEST

GATHER_BITS = {"tgt": (1, 2, 0), "src": (2, 1, 3, 0)}
SCATTER_BITS = {"tgt": (0, 2, 1), "src": (0, 3, 1, 2)}


def partner(axis, n, bit):
    return [(i, i ^ (1 << bit)) for i in range(n)]


def axis_size(axis):
    return lax.axis_size(axis)


def tree_sum(x, axis):
    n = axis_size(axis)
    for bit in range(n.bit_length() - 1):
        x = x + lax.ppermute(x, axis, partner(axis, n, bit))
    return x


def tree_gather(x, axis, order):
    n = axis_size(axis)
    me = lax.axis_index(axis)
    for bit in order:
        other = lax.ppermute(x, axis, partner(axis, n, bit))
        up = ((me >> bit) & 1) == 1
        x = jnp.where(up, jnp.stack([other, x]), jnp.stack([x, other]))
    held = list(reversed(order))
    perm = [held.index(b) for b in reversed(range(len(order)))]
    x = jnp.transpose(x, perm + list(range(len(order), x.ndim)))
    return x.reshape((n * x.shape[len(order)],) + x.shape[len(order) + 1:])


def tree_scatter(x, axis, order):
    n = axis_size(axis)
    me = lax.axis_index(axis)
    k = len(order)
    rows = x.shape[0] // n
    x = x.reshape((2,) * k + (rows,) + x.shape[1:])
    held = list(reversed(range(k)))
    for bit in order:
        a = held.index(bit)
        lo = lax.index_in_dim(x, 0, a, keepdims=False)
        hi = lax.index_in_dim(x, 1, a, keepdims=False)
        up = ((me >> bit) & 1) == 1
        keep = jnp.where(up, hi, lo)
        send = jnp.where(up, lo, hi)
        x = keep + lax.ppermute(send, axis, partner(axis, n, bit))
        held.pop(a)
    return x


def row_total(part):
    return tree_sum(part, "tgt")


def col_total(part):
    return tree_sum(part, "src")


def times_vector(kernel, vector):
    return jnp.dot(kernel, vector, precision=highest, preferred_element_type=jnp.float32)


def vector_times(vector, kernel):
    return jnp.dot(vector, kernel, precision=highest, preferred_element_type=jnp.float32)


def per_device(src_emb, right_sentence_vectors, src_mass, tgt_mass):
    src_rows = tree_gather(src_emb, "tgt", GATHER_BITS["tgt"])
    target_rows = tree_gather(right_sentence_vectors, "src", GATHER_BITS["src"])

    kernel_grid = (
        lax.dot_general(
            src_rows, target_rows, (((1,), (1,)), ((), ())), preferred_element_type=jnp.float32
        )
        / regularizer_epsilon
    )
    kernel = lax.optimization_barrier(jnp.exp(kernel_grid).astype(jnp.bfloat16))
    weighted = kernel * kernel_grid

    vector = jnp.ones(tgt_mass.shape, jnp.float32)
    old_saved, row_saved, src_saved, col_saved, tgt_saved = ([], [], [], [], [])
    tgt_adj = None
    for iteration in range(ITERS):
        old_saved.append(vector)
        row_sum = row_total(times_vector(kernel, vector))
        src_scale = src_mass / row_sum
        if iteration == ITERS - 1:
            both = col_total(
                jnp.stack([vector_times(src_scale, kernel), vector_times(src_scale, weighted)])
            )
            col_sum, tgt_adj = both[0], both[1]
        else:
            col_sum = col_total(vector_times(src_scale, kernel))
        vector = tgt_mass / col_sum
        row_saved.append(row_sum)
        src_saved.append(src_scale)
        col_saved.append(col_sum)
        tgt_saved.append(vector)
    last_src = src_saved[-1]
    last_tgt = tgt_saved[-1]
    row_bars = [None] * ITERS
    col_bars = [None] * ITERS
    for iteration in reversed(range(ITERS)):
        col_bar = -tgt_adj * tgt_saved[iteration] / col_saved[iteration]
        part = times_vector(kernel, col_bar)
        if iteration == ITERS - 1:
            part = part + times_vector(weighted, last_tgt)
        back = row_total(part)
        row_bar = -back * src_saved[iteration] / row_saved[iteration]
        if iteration > 0:
            tgt_adj = col_total(vector_times(row_bar, kernel))
        row_bars[iteration] = row_bar
        col_bars[iteration] = col_bar
    left = jnp.stack(row_bars + src_saved, axis=1)
    right = jnp.stack(old_saved + col_bars, axis=1)
    lowrank = lax.dot_general(
        left, right, (((1,), (1,)), ((), ())), precision=highest, preferred_element_type=jnp.float32
    )
    cross_term_grid = (
        kernel * (last_src[:, None] * last_tgt[None, :] * (1.0 + kernel_grid) + lowrank)
    ).astype(jnp.bfloat16)
    left_share_piece = (
        jnp.dot(cross_term_grid, target_rows, preferred_element_type=jnp.float32)
        / regularizer_epsilon
    )
    right_share_piece = (
        lax.dot_general(
            cross_term_grid, src_rows, (((0,), (0,)), ((), ())), preferred_element_type=jnp.float32
        )
        / regularizer_epsilon
    )
    grad_src = tree_scatter(left_share_piece, "tgt", SCATTER_BITS["tgt"])
    grad_tgt = tree_scatter(right_share_piece, "src", SCATTER_BITS["src"])
    return (grad_src, grad_tgt)


def solution(mesh):
    placed = (P(("src", "tgt"), None), P(("tgt", "src"), None), P("src"), P("tgt"))
    return jax.shard_map(
        per_device,
        mesh=mesh,
        in_specs=placed,
        out_specs=(P(("src", "tgt"), None), P(("tgt", "src"), None)),
        check_vma=False,
    )
```

```python
import jax
import jax.numpy as jnp
from jax import lax
from jax.sharding import PartitionSpec as P

ITERS = 4


regularizer_epsilon = 0.05
highest = lax.Precision.HIGHEST

GATHER_BITS = {"tgt": (1, 2, 0), "src": (2, 1, 3, 0)}
SCATTER_BITS = {"tgt": (0, 2, 1), "src": (0, 3, 1, 2)}


def partner(axis, n, bit):
    return [(i, i ^ (1 << bit)) for i in range(n)]


def axis_size(axis):
    return lax.axis_size(axis)


def tree_sum(x, axis):
    n = axis_size(axis)
    spread = jnp.broadcast_to(x[None], (n,) + x.shape)
    return lax.all_to_all(spread, axis, 0, 0, tiled=False).sum(0)


def tree_gather(x, axis, order):
    n = axis_size(axis)
    me = lax.axis_index(axis)
    for bit in order:
        other = lax.ppermute(x, axis, partner(axis, n, bit))
        up = ((me >> bit) & 1) == 1
        x = jnp.where(up, jnp.stack([other, x]), jnp.stack([x, other]))
    held = list(reversed(order))
    perm = [held.index(b) for b in reversed(range(len(order)))]
    x = jnp.transpose(x, perm + list(range(len(order), x.ndim)))
    return x.reshape((n * x.shape[len(order)],) + x.shape[len(order) + 1:])


def tree_scatter(x, axis, order):
    n = axis_size(axis)
    me = lax.axis_index(axis)
    k = len(order)
    rows = x.shape[0] // n
    x = x.reshape((2,) * k + (rows,) + x.shape[1:])
    held = list(reversed(range(k)))
    for bit in order:
        a = held.index(bit)
        lo = lax.index_in_dim(x, 0, a, keepdims=False)
        hi = lax.index_in_dim(x, 1, a, keepdims=False)
        up = ((me >> bit) & 1) == 1
        keep = jnp.where(up, hi, lo)
        send = jnp.where(up, lo, hi)
        x = keep + lax.ppermute(send, axis, partner(axis, n, bit))
        held.pop(a)
    return x


def row_total(part):
    return tree_sum(part, "tgt")


def col_total(part):
    return tree_sum(part, "src")


def times_vector(kernel, vector):
    return jnp.dot(kernel, vector, precision=highest, preferred_element_type=jnp.float32)


def vector_times(vector, kernel):
    return jnp.dot(vector, kernel, precision=highest, preferred_element_type=jnp.float32)


def per_device(src_emb, right_sentence_vectors, src_mass, tgt_mass):
    src_rows = tree_gather(src_emb, "tgt", GATHER_BITS["tgt"])
    target_rows = tree_gather(right_sentence_vectors, "src", GATHER_BITS["src"])

    kernel_grid = (
        lax.dot_general(
            src_rows, target_rows, (((1,), (1,)), ((), ())), preferred_element_type=jnp.float32
        )
        / regularizer_epsilon
    )
    kernel = lax.optimization_barrier(jnp.exp(kernel_grid).astype(jnp.bfloat16))
    weighted = kernel * kernel_grid

    vector = jnp.ones(tgt_mass.shape, jnp.float32)
    old_saved, row_saved, src_saved, col_saved, tgt_saved = ([], [], [], [], [])
    tgt_adj = None
    for iteration in range(ITERS):
        old_saved.append(vector)
        row_sum = row_total(times_vector(kernel, vector))
        src_scale = src_mass / row_sum
        if iteration == ITERS - 1:
            both = col_total(
                jnp.stack([vector_times(src_scale, kernel), vector_times(src_scale, weighted)])
            )
            col_sum, tgt_adj = both[0], both[1]
        else:
            col_sum = col_total(vector_times(src_scale, kernel))
        vector = tgt_mass / col_sum
        row_saved.append(row_sum)
        src_saved.append(src_scale)
        col_saved.append(col_sum)
        tgt_saved.append(vector)
    last_src = src_saved[-1]
    last_tgt = tgt_saved[-1]
    row_bars = [None] * ITERS
    col_bars = [None] * ITERS
    for iteration in reversed(range(ITERS)):
        col_bar = -tgt_adj * tgt_saved[iteration] / col_saved[iteration]
        part = times_vector(kernel, col_bar)
        if iteration == ITERS - 1:
            part = part + times_vector(weighted, last_tgt)
        back = row_total(part)
        row_bar = -back * src_saved[iteration] / row_saved[iteration]
        if iteration > 0:
            tgt_adj = col_total(vector_times(row_bar, kernel))
        row_bars[iteration] = row_bar
        col_bars[iteration] = col_bar
    left = jnp.stack(row_bars + src_saved, axis=1)
    right = jnp.stack(old_saved + col_bars, axis=1)
    lowrank = lax.dot_general(
        left, right, (((1,), (1,)), ((), ())), precision=highest, preferred_element_type=jnp.float32
    )
    cross_term_grid = (
        kernel * (last_src[:, None] * last_tgt[None, :] * (1.0 + kernel_grid) + lowrank)
    ).astype(jnp.bfloat16)
    left_share_piece = (
        jnp.dot(cross_term_grid, target_rows, preferred_element_type=jnp.float32)
        / regularizer_epsilon
    )
    right_share_piece = (
        lax.dot_general(
            cross_term_grid, src_rows, (((0,), (0,)), ((), ())), preferred_element_type=jnp.float32
        )
        / regularizer_epsilon
    )
    grad_src = tree_scatter(left_share_piece, "tgt", SCATTER_BITS["tgt"])
    grad_tgt = tree_scatter(right_share_piece, "src", SCATTER_BITS["src"])
    return (grad_src, grad_tgt)


def solution(mesh):
    placed = (P(("src", "tgt"), None), P(("tgt", "src"), None), P("src"), P("tgt"))
    return jax.shard_map(
        per_device,
        mesh=mesh,
        in_specs=placed,
        out_specs=(P(("src", "tgt"), None), P(("tgt", "src"), None)),
        check_vma=False,
    )
```

```python
import jax
import jax.numpy as jnp
from jax import lax
from jax.sharding import PartitionSpec as P

ITERS = 4


regularizer_epsilon = 0.05
highest = lax.Precision.HIGHEST

GATHER_BITS = {"tgt": ((1, 2, 0), (1, 0, 2)), "src": ((2, 1, 3, 0), (2, 3, 1, 0))}
SCATTER_BITS = {"tgt": ((0, 2, 1), (2, 0, 1)), "src": ((0, 3, 1, 2), (0, 1, 3, 2))}


def partner(axis, n, bit):
    return [(i, i ^ (1 << bit)) for i in range(n)]


def axis_size(axis):
    return lax.axis_size(axis)


def tree_sum(x, axis):
    n = axis_size(axis)
    spread = jnp.broadcast_to(x[None], (n,) + x.shape)
    return lax.all_to_all(spread, axis, 0, 0, tiled=False).sum(0)


def tree_gather(x, axis, order):
    n = axis_size(axis)
    me = lax.axis_index(axis)
    for bit in order:
        other = lax.ppermute(x, axis, partner(axis, n, bit))
        up = ((me >> bit) & 1) == 1
        x = jnp.where(up, jnp.stack([other, x]), jnp.stack([x, other]))
    held = list(reversed(order))
    perm = [held.index(b) for b in reversed(range(len(order)))]
    x = jnp.transpose(x, perm + list(range(len(order), x.ndim)))
    return x.reshape((n * x.shape[len(order)],) + x.shape[len(order) + 1:])


def tree_scatter(x, axis, order):
    n = axis_size(axis)
    me = lax.axis_index(axis)
    k = len(order)
    rows = x.shape[0] // n
    x = x.reshape((2,) * k + (rows,) + x.shape[1:])
    held = list(reversed(range(k)))
    for bit in order:
        a = held.index(bit)
        lo = lax.index_in_dim(x, 0, a, keepdims=False)
        hi = lax.index_in_dim(x, 1, a, keepdims=False)
        up = ((me >> bit) & 1) == 1
        keep = jnp.where(up, hi, lo)
        send = jnp.where(up, lo, hi)
        x = keep + lax.ppermute(send, axis, partner(axis, n, bit))
        held.pop(a)
    return x


def split_gather(x, axis):
    orders = GATHER_BITS[axis]
    w = x.shape[1] // len(orders)
    return jnp.concatenate(
        [tree_gather(x[:, i * w:(i + 1) * w], axis, o) for i, o in enumerate(orders)], 1
    )


def split_scatter(x, axis):
    orders = SCATTER_BITS[axis]
    w = x.shape[1] // len(orders)
    return jnp.concatenate(
        [tree_scatter(x[:, i * w:(i + 1) * w], axis, o) for i, o in enumerate(orders)], 1
    )


def row_total(part):
    return tree_sum(part, "tgt")


def col_total(part):
    return tree_sum(part, "src")


def times_vector(kernel, vector):
    return jnp.dot(kernel, vector, precision=highest, preferred_element_type=jnp.float32)


def vector_times(vector, kernel):
    return jnp.dot(vector, kernel, precision=highest, preferred_element_type=jnp.float32)


def per_device(src_emb, right_sentence_vectors, src_mass, tgt_mass):
    src_rows = split_gather(src_emb, "tgt")
    target_rows = split_gather(right_sentence_vectors, "src")

    kernel_grid = (
        lax.dot_general(
            src_rows, target_rows, (((1,), (1,)), ((), ())), preferred_element_type=jnp.float32
        )
        / regularizer_epsilon
    )
    kernel = lax.optimization_barrier(jnp.exp(kernel_grid).astype(jnp.bfloat16))
    weighted = kernel * kernel_grid

    vector = jnp.ones(tgt_mass.shape, jnp.float32)
    old_saved, row_saved, src_saved, col_saved, tgt_saved = ([], [], [], [], [])
    tgt_adj = None
    for iteration in range(ITERS):
        old_saved.append(vector)
        row_sum = row_total(times_vector(kernel, vector))
        src_scale = src_mass / row_sum
        if iteration == ITERS - 1:
            both = col_total(
                jnp.stack([vector_times(src_scale, kernel), vector_times(src_scale, weighted)])
            )
            col_sum, tgt_adj = both[0], both[1]
        else:
            col_sum = col_total(vector_times(src_scale, kernel))
        vector = tgt_mass / col_sum
        row_saved.append(row_sum)
        src_saved.append(src_scale)
        col_saved.append(col_sum)
        tgt_saved.append(vector)
    last_src = src_saved[-1]
    last_tgt = tgt_saved[-1]
    row_bars = [None] * ITERS
    col_bars = [None] * ITERS
    for iteration in reversed(range(ITERS)):
        col_bar = -tgt_adj * tgt_saved[iteration] / col_saved[iteration]
        part = times_vector(kernel, col_bar)
        if iteration == ITERS - 1:
            part = part + times_vector(weighted, last_tgt)
        back = row_total(part)
        row_bar = -back * src_saved[iteration] / row_saved[iteration]
        if iteration > 0:
            tgt_adj = col_total(vector_times(row_bar, kernel))
        row_bars[iteration] = row_bar
        col_bars[iteration] = col_bar
    left = jnp.stack(row_bars + src_saved, axis=1)
    right = jnp.stack(old_saved + col_bars, axis=1)
    lowrank = lax.dot_general(
        left, right, (((1,), (1,)), ((), ())), precision=highest, preferred_element_type=jnp.float32
    )
    cross_term_grid = (
        kernel * (last_src[:, None] * last_tgt[None, :] * (1.0 + kernel_grid) + lowrank)
    ).astype(jnp.bfloat16)
    left_share_piece = (
        jnp.dot(cross_term_grid, target_rows, preferred_element_type=jnp.float32)
        / regularizer_epsilon
    )
    right_share_piece = (
        lax.dot_general(
            cross_term_grid, src_rows, (((0,), (0,)), ((), ())), preferred_element_type=jnp.float32
        )
        / regularizer_epsilon
    )
    grad_src = split_scatter(left_share_piece, "tgt")
    grad_tgt = split_scatter(right_share_piece, "src")
    return (grad_src, grad_tgt)


def solution(mesh):
    placed = (P(("src", "tgt"), None), P(("tgt", "src"), None), P("src"), P("tgt"))
    return jax.shard_map(
        per_device,
        mesh=mesh,
        in_specs=placed,
        out_specs=(P(("src", "tgt"), None), P(("tgt", "src"), None)),
        check_vma=False,
    )
```

```python
import jax
import jax.numpy as jnp
from jax import lax
from jax.sharding import PartitionSpec as P

ITERS = 4


regularizer_epsilon = 0.05
highest = lax.Precision.HIGHEST

GATHER_BITS = {"tgt": ((1, 2, 0), (1, 0, 2)), "src": ((2, 1, 3, 0), (2, 3, 1, 0))}
SCATTER_BITS = {"tgt": ((0, 2, 1), (2, 0, 1)), "src": ((0, 3, 1, 2), (0, 1, 3, 2))}


def partner(axis, n, bit):
    return [(i, i ^ (1 << bit)) for i in range(n)]


def axis_size(axis):
    return lax.axis_size(axis)


def tree_sum(x, axis):
    n = axis_size(axis)
    spread = jnp.broadcast_to(x[None], (n,) + x.shape)
    return lax.all_to_all(spread, axis, 0, 0, tiled=False).sum(0)


def tree_gather(x, axis, order):
    n = axis_size(axis)
    me = lax.axis_index(axis)
    for bit in order:
        other = lax.ppermute(x, axis, partner(axis, n, bit))
        up = ((me >> bit) & 1) == 1
        x = jnp.where(up, jnp.stack([other, x]), jnp.stack([x, other]))
    held = list(reversed(order))
    perm = [held.index(b) for b in reversed(range(len(order)))]
    x = jnp.transpose(x, perm + list(range(len(order), x.ndim)))
    return x.reshape((n * x.shape[len(order)],) + x.shape[len(order) + 1:])


def tree_scatter(x, axis, order):
    n = axis_size(axis)
    me = lax.axis_index(axis)
    k = len(order)
    rows = x.shape[0] // n
    x = x.reshape((2,) * k + (rows,) + x.shape[1:])
    held = list(reversed(range(k)))
    for bit in order:
        a = held.index(bit)
        lo = lax.index_in_dim(x, 0, a, keepdims=False)
        hi = lax.index_in_dim(x, 1, a, keepdims=False)
        up = ((me >> bit) & 1) == 1
        keep = jnp.where(up, hi, lo)
        send = jnp.where(up, lo, hi)
        x = keep + lax.ppermute(send, axis, partner(axis, n, bit))
        held.pop(a)
    return x


def split_gather(x, axis):
    orders = GATHER_BITS[axis]
    w = x.shape[1] // len(orders)
    return jnp.concatenate(
        [tree_gather(x[:, i * w:(i + 1) * w], axis, o) for i, o in enumerate(orders)], 1
    )


def split_scatter(x, axis):
    orders = SCATTER_BITS[axis]
    w = x.shape[1] // len(orders)
    return jnp.concatenate(
        [tree_scatter(x[:, i * w:(i + 1) * w], axis, o) for i, o in enumerate(orders)], 1
    )


def row_total(part):
    return tree_sum(part, "tgt")


def col_total(part):
    return tree_sum(part, "src")


def times_vector(kernel, vector):
    return jnp.sum(kernel.astype(jnp.float32) * vector[None, :], axis=1)


def vector_times(vector, kernel):
    return jnp.sum(vector[:, None] * kernel.astype(jnp.float32), axis=0)


def per_device(src_emb, right_sentence_vectors, src_mass, tgt_mass):
    src_rows = split_gather(src_emb, "tgt")
    target_rows = split_gather(right_sentence_vectors, "src")

    kernel_grid = (
        lax.dot_general(
            src_rows, target_rows, (((1,), (1,)), ((), ())), preferred_element_type=jnp.float32
        )
        / regularizer_epsilon
    )
    kernel = lax.optimization_barrier(jnp.exp(kernel_grid).astype(jnp.bfloat16))
    weighted = kernel * kernel_grid

    vector = jnp.ones(tgt_mass.shape, jnp.float32)
    old_saved, row_saved, src_saved, col_saved, tgt_saved = ([], [], [], [], [])
    tgt_adj = None
    for iteration in range(ITERS):
        old_saved.append(vector)
        row_sum = row_total(times_vector(kernel, vector))
        src_scale = src_mass / row_sum
        if iteration == ITERS - 1:
            both = col_total(
                jnp.stack([vector_times(src_scale, kernel), vector_times(src_scale, weighted)])
            )
            col_sum, tgt_adj = both[0], both[1]
        else:
            col_sum = col_total(vector_times(src_scale, kernel))
        vector = tgt_mass / col_sum
        row_saved.append(row_sum)
        src_saved.append(src_scale)
        col_saved.append(col_sum)
        tgt_saved.append(vector)
    last_src = src_saved[-1]
    last_tgt = tgt_saved[-1]
    row_bars = [None] * ITERS
    col_bars = [None] * ITERS
    for iteration in reversed(range(ITERS)):
        col_bar = -tgt_adj * tgt_saved[iteration] / col_saved[iteration]
        part = times_vector(kernel, col_bar)
        if iteration == ITERS - 1:
            part = part + times_vector(weighted, last_tgt)
        back = row_total(part)
        row_bar = -back * src_saved[iteration] / row_saved[iteration]
        if iteration > 0:
            tgt_adj = col_total(vector_times(row_bar, kernel))
        row_bars[iteration] = row_bar
        col_bars[iteration] = col_bar
    left = jnp.stack(row_bars + src_saved, axis=1)
    right = jnp.stack(old_saved + col_bars, axis=1)
    lowrank = lax.dot_general(
        left, right, (((1,), (1,)), ((), ())), precision=highest, preferred_element_type=jnp.float32
    )
    cross_term_grid = (
        kernel * (last_src[:, None] * last_tgt[None, :] * (1.0 + kernel_grid) + lowrank)
    ).astype(jnp.bfloat16)
    left_share_piece = (
        jnp.dot(cross_term_grid, target_rows, preferred_element_type=jnp.float32)
        / regularizer_epsilon
    )
    right_share_piece = (
        lax.dot_general(
            cross_term_grid, src_rows, (((0,), (0,)), ((), ())), preferred_element_type=jnp.float32
        )
        / regularizer_epsilon
    )
    grad_src = split_scatter(left_share_piece, "tgt")
    grad_tgt = split_scatter(right_share_piece, "src")
    return (grad_src, grad_tgt)


def solution(mesh):
    placed = (P(("src", "tgt"), None), P(("tgt", "src"), None), P("src"), P("tgt"))
    return jax.shard_map(
        per_device,
        mesh=mesh,
        in_specs=placed,
        out_specs=(P(("src", "tgt"), None), P(("tgt", "src"), None)),
        check_vma=False,
    )
```

```python
import jax
import jax.numpy as jnp
from jax import lax
from jax.sharding import PartitionSpec as P

ITERS = 4


regularizer_epsilon = 0.05
highest = lax.Precision.HIGHEST

GATHER_BITS = {"tgt": ((1, 2, 0), (1, 0, 2)), "src": ((2, 1, 3, 0), (2, 3, 1, 0))}
SCATTER_BITS = {"tgt": ((0, 2, 1), (2, 0, 1)), "src": ((0, 3, 1, 2), (0, 1, 3, 2))}


def partner(axis, n, bit):
    return [(i, i ^ (1 << bit)) for i in range(n)]


def axis_size(axis):
    return lax.axis_size(axis)


def tree_sum(x, axis):
    n = axis_size(axis)
    spread = jnp.broadcast_to(x[None], (n,) + x.shape)
    return lax.all_to_all(spread, axis, 0, 0, tiled=False).sum(0)


def tree_gather(x, axis, order):
    n = axis_size(axis)
    me = lax.axis_index(axis)
    for bit in order:
        other = lax.ppermute(x, axis, partner(axis, n, bit))
        up = ((me >> bit) & 1) == 1
        x = jnp.where(up, jnp.stack([other, x]), jnp.stack([x, other]))
    held = list(reversed(order))
    perm = [held.index(b) for b in reversed(range(len(order)))]
    x = jnp.transpose(x, perm + list(range(len(order), x.ndim)))
    return x.reshape((n * x.shape[len(order)],) + x.shape[len(order) + 1:])


def tree_scatter(x, axis, order):
    n = axis_size(axis)
    me = lax.axis_index(axis)
    k = len(order)
    rows = x.shape[0] // n
    x = x.reshape((2,) * k + (rows,) + x.shape[1:])
    held = list(reversed(range(k)))
    for bit in order:
        a = held.index(bit)
        lo = lax.index_in_dim(x, 0, a, keepdims=False)
        hi = lax.index_in_dim(x, 1, a, keepdims=False)
        up = ((me >> bit) & 1) == 1
        keep = jnp.where(up, hi, lo)
        send = jnp.where(up, lo, hi)
        x = keep + lax.ppermute(send, axis, partner(axis, n, bit))
        held.pop(a)
    return x


def split_gather(x, axis):
    orders = GATHER_BITS[axis]
    w = x.shape[1] // len(orders)
    return jnp.concatenate(
        [tree_gather(x[:, i * w:(i + 1) * w], axis, o) for i, o in enumerate(orders)], 1
    )


def split_scatter(x, axis):
    orders = SCATTER_BITS[axis]
    w = x.shape[1] // len(orders)
    return jnp.concatenate(
        [tree_scatter(x[:, i * w:(i + 1) * w], axis, o) for i, o in enumerate(orders)], 1
    )


def row_total(part):
    return tree_sum(part, "tgt")


def col_total(part):
    return tree_sum(part, "src")


def times_vector(kernel, vector):
    return jnp.sum(kernel.astype(jnp.float32) * vector[None, :], axis=1)


def vector_times(vector, kernel):
    return jnp.sum(vector[:, None] * kernel.astype(jnp.float32), axis=0)


def per_device(src_emb, right_sentence_vectors, src_mass, tgt_mass):
    src_rows = split_gather(src_emb, "tgt")
    target_rows = split_gather(right_sentence_vectors, "src")

    kernel_grid = (
        lax.dot_general(
            src_rows, target_rows, (((1,), (1,)), ((), ())), preferred_element_type=jnp.float32
        )
        / regularizer_epsilon
    )
    kernel = lax.optimization_barrier(jnp.exp(kernel_grid).astype(jnp.bfloat16))
    weighted = kernel * kernel_grid

    vector = jnp.ones(tgt_mass.shape, jnp.float32)
    old_saved, row_saved, src_saved, col_saved, tgt_saved = ([], [], [], [], [])
    tgt_adj = None
    for iteration in range(ITERS):
        old_saved.append(vector)
        row_sum = row_total(times_vector(kernel, vector))
        src_scale = src_mass / row_sum
        if iteration == ITERS - 1:
            both = col_total(
                jnp.stack([vector_times(src_scale, kernel), vector_times(src_scale, weighted)])
            )
            col_sum, tgt_adj = both[0], both[1]
        else:
            col_sum = col_total(vector_times(src_scale, kernel))
        vector = tgt_mass / col_sum
        row_saved.append(row_sum)
        src_saved.append(src_scale)
        col_saved.append(col_sum)
        tgt_saved.append(vector)
    last_src = src_saved[-1]
    last_tgt = tgt_saved[-1]
    row_bars = [None] * ITERS
    col_bars = [None] * ITERS
    for iteration in reversed(range(ITERS)):
        col_bar = -tgt_adj * tgt_saved[iteration] / col_saved[iteration]
        part = times_vector(kernel, col_bar)
        if iteration == ITERS - 1:
            part = part + times_vector(weighted, last_tgt)
        back = row_total(part)
        row_bar = -back * src_saved[iteration] / row_saved[iteration]
        if iteration > 0:
            tgt_adj = col_total(vector_times(row_bar, kernel))
        row_bars[iteration] = row_bar
        col_bars[iteration] = col_bar
    left = jnp.stack(row_bars + src_saved, axis=1)
    right = jnp.stack(old_saved + col_bars, axis=1)
    lowrank = left[:, 0, None] * right[None, :, 0]
    for k in range(1, left.shape[1]):
        lowrank = lowrank + left[:, k, None] * right[None, :, k]
    cross_term_grid = (
        kernel * (last_src[:, None] * last_tgt[None, :] * (1.0 + kernel_grid) + lowrank)
    ).astype(jnp.bfloat16)
    left_share_piece = (
        jnp.dot(cross_term_grid, target_rows, preferred_element_type=jnp.float32)
        / regularizer_epsilon
    )
    right_share_piece = (
        lax.dot_general(
            cross_term_grid, src_rows, (((0,), (0,)), ((), ())), preferred_element_type=jnp.float32
        )
        / regularizer_epsilon
    )
    grad_src = split_scatter(left_share_piece, "tgt")
    grad_tgt = split_scatter(right_share_piece, "src")
    return (grad_src, grad_tgt)


def solution(mesh):
    placed = (P(("src", "tgt"), None), P(("tgt", "src"), None), P("src"), P("tgt"))
    return jax.shard_map(
        per_device,
        mesh=mesh,
        in_specs=placed,
        out_specs=(P(("src", "tgt"), None), P(("tgt", "src"), None)),
        check_vma=False,
    )
```

```python
import jax
import jax.numpy as jnp
from jax import lax
from jax.sharding import PartitionSpec as P

ITERS = 4


regularizer_epsilon = 0.05
highest = lax.Precision.HIGHEST

GATHER_BITS = {"tgt": ((1, 2, 0), (1, 0, 2)), "src": ((2, 1, 3, 0), (2, 3, 1, 0))}
SCATTER_BITS = {"tgt": ((0, 2, 1), (2, 0, 1)), "src": ((0, 3, 1, 2), (0, 1, 3, 2))}


def partner(axis, n, bit):
    return [(i, i ^ (1 << bit)) for i in range(n)]


def axis_size(axis):
    return lax.axis_size(axis)


def tree_sum(x, axis):
    n = axis_size(axis)
    spread = jnp.broadcast_to(x[None], (n,) + x.shape)
    return lax.all_to_all(spread, axis, 0, 0, tiled=False).sum(0)


def tree_gather(x, axis, order):
    n = axis_size(axis)
    me = lax.axis_index(axis)
    for bit in order:
        other = lax.ppermute(x, axis, partner(axis, n, bit))
        up = ((me >> bit) & 1) == 1
        x = jnp.where(up, jnp.stack([other, x]), jnp.stack([x, other]))
    held = list(reversed(order))
    perm = [held.index(b) for b in reversed(range(len(order)))]
    x = jnp.transpose(x, perm + list(range(len(order), x.ndim)))
    return x.reshape((n * x.shape[len(order)],) + x.shape[len(order) + 1:])


def tree_scatter(x, axis, order):
    n = axis_size(axis)
    me = lax.axis_index(axis)
    k = len(order)
    rows = x.shape[0] // n
    x = x.reshape((2,) * k + (rows,) + x.shape[1:])
    held = list(reversed(range(k)))
    for bit in order:
        a = held.index(bit)
        lo = lax.index_in_dim(x, 0, a, keepdims=False)
        hi = lax.index_in_dim(x, 1, a, keepdims=False)
        up = ((me >> bit) & 1) == 1
        keep = jnp.where(up, hi, lo)
        send = jnp.where(up, lo, hi)
        x = keep + lax.ppermute(send, axis, partner(axis, n, bit))
        held.pop(a)
    return x


def split_gather(x, axis):
    orders = GATHER_BITS[axis]
    w = x.shape[1] // len(orders)
    return jnp.concatenate(
        [tree_gather(x[:, i * w:(i + 1) * w], axis, o) for i, o in enumerate(orders)], 1
    )


def split_scatter(x, axis):
    orders = SCATTER_BITS[axis]
    w = x.shape[1] // len(orders)
    return jnp.concatenate(
        [tree_scatter(x[:, i * w:(i + 1) * w], axis, o) for i, o in enumerate(orders)], 1
    )


def to_bf16_grid(x):
    return lax.reduce_precision(x, exponent_bits=8, mantissa_bits=7)


def split3(x):
    high = to_bf16_grid(x)
    rest = x - high
    mid = to_bf16_grid(rest)
    low = rest - mid
    return [p.astype(jnp.bfloat16) for p in (high, mid, low)]


def row_total(part):
    return tree_sum(part, "tgt")


def col_total(part):
    return tree_sum(part, "src")


def times_vector(kernel, vector):
    return jnp.sum(kernel.astype(jnp.float32) * vector[None, :], axis=1)


def vector_times(vector, kernel):
    return jnp.sum(vector[:, None] * kernel.astype(jnp.float32), axis=0)


def per_device(src_emb, right_sentence_vectors, src_mass, tgt_mass):
    src_rows = split_gather(src_emb, "tgt")
    target_rows = split_gather(right_sentence_vectors, "src")

    kernel_grid = (
        lax.dot_general(
            src_rows, target_rows, (((1,), (1,)), ((), ())), preferred_element_type=jnp.float32
        )
        / regularizer_epsilon
    )
    kernel = lax.optimization_barrier(jnp.exp(kernel_grid).astype(jnp.bfloat16))
    weighted = kernel * kernel_grid

    vector = jnp.ones(tgt_mass.shape, jnp.float32)
    old_saved, row_saved, src_saved, col_saved, tgt_saved = ([], [], [], [], [])
    tgt_adj = None
    for iteration in range(ITERS):
        old_saved.append(vector)
        row_sum = row_total(times_vector(kernel, vector))
        src_scale = src_mass / row_sum
        if iteration == ITERS - 1:
            both = col_total(
                jnp.stack([vector_times(src_scale, kernel), vector_times(src_scale, weighted)])
            )
            col_sum, tgt_adj = both[0], both[1]
        else:
            col_sum = col_total(vector_times(src_scale, kernel))
        vector = tgt_mass / col_sum
        row_saved.append(row_sum)
        src_saved.append(src_scale)
        col_saved.append(col_sum)
        tgt_saved.append(vector)
    last_src = src_saved[-1]
    last_tgt = tgt_saved[-1]
    row_bars = [None] * ITERS
    col_bars = [None] * ITERS
    for iteration in reversed(range(ITERS)):
        col_bar = -tgt_adj * tgt_saved[iteration] / col_saved[iteration]
        part = times_vector(kernel, col_bar)
        if iteration == ITERS - 1:
            part = part + times_vector(weighted, last_tgt)
        back = row_total(part)
        row_bar = -back * src_saved[iteration] / row_saved[iteration]
        if iteration > 0:
            tgt_adj = col_total(vector_times(row_bar, kernel))
        row_bars[iteration] = row_bar
        col_bars[iteration] = col_bar
    left = jnp.stack(row_bars + src_saved, axis=1)
    right = jnp.stack(old_saved + col_bars, axis=1)
    left_pieces, right_pieces = split3(left), split3(right)
    left_all = jnp.concatenate([a for a in left_pieces for b in right_pieces], axis=1)
    right_all = jnp.concatenate([b for a in left_pieces for b in right_pieces], axis=1)
    lowrank = lax.dot_general(
        left_all, right_all, (((1,), (1,)), ((), ())), preferred_element_type=jnp.float32
    )
    cross_term_grid = (
        kernel * (last_src[:, None] * last_tgt[None, :] * (1.0 + kernel_grid) + lowrank)
    ).astype(jnp.bfloat16)
    left_share_piece = (
        jnp.dot(cross_term_grid, target_rows, preferred_element_type=jnp.float32)
        / regularizer_epsilon
    )
    right_share_piece = (
        lax.dot_general(
            cross_term_grid, src_rows, (((0,), (0,)), ((), ())), preferred_element_type=jnp.float32
        )
        / regularizer_epsilon
    )
    grad_src = split_scatter(left_share_piece, "tgt")
    grad_tgt = split_scatter(right_share_piece, "src")
    return (grad_src, grad_tgt)


def solution(mesh):
    placed = (P(("src", "tgt"), None), P(("tgt", "src"), None), P("src"), P("tgt"))
    return jax.shard_map(
        per_device,
        mesh=mesh,
        in_specs=placed,
        out_specs=(P(("src", "tgt"), None), P(("tgt", "src"), None)),
        check_vma=False,
    )
```

```python
import jax
import jax.numpy as jnp
from jax import lax
from jax.sharding import Mesh, PartitionSpec as P

ITERS = 4


regularizer_epsilon = 0.05
highest = lax.Precision.HIGHEST

PHYSICAL = ("y_lo", "z", "core", "y_hi", "x")
ROWS = ("y_lo", "core", "y_hi")
COLS = ("z", "x")

GATHER_BITS = {ROWS: ((0, 2, 1), (2, 0, 1)), COLS: ((1, 3, 2, 0), (3, 1, 0, 2))}
SCATTER_BITS = {ROWS: ((1, 2, 0), (1, 0, 2)), COLS: ((0, 2, 1, 3), (2, 0, 3, 1))}


def partner(axis, n, bit):
    return [(i, i ^ (1 << bit)) for i in range(n)]


def axis_size(axis):
    return lax.axis_size(axis)


def tree_sum(x, axis):
    n = axis_size(axis)
    spread = jnp.broadcast_to(x[None], (n,) + x.shape)
    return lax.all_to_all(spread, axis, 0, 0, tiled=False).sum(0)


def tree_gather(x, axis, order):
    n = axis_size(axis)
    me = lax.axis_index(axis)
    for bit in order:
        other = lax.ppermute(x, axis, partner(axis, n, bit))
        up = ((me >> bit) & 1) == 1
        x = jnp.where(up, jnp.stack([other, x]), jnp.stack([x, other]))
    held = list(reversed(order))
    perm = [held.index(b) for b in reversed(range(len(order)))]
    x = jnp.transpose(x, perm + list(range(len(order), x.ndim)))
    return x.reshape((n * x.shape[len(order)],) + x.shape[len(order) + 1:])


def tree_scatter(x, axis, order):
    n = axis_size(axis)
    me = lax.axis_index(axis)
    k = len(order)
    rows = x.shape[0] // n
    x = x.reshape((2,) * k + (rows,) + x.shape[1:])
    held = list(reversed(range(k)))
    for bit in order:
        a = held.index(bit)
        lo = lax.index_in_dim(x, 0, a, keepdims=False)
        hi = lax.index_in_dim(x, 1, a, keepdims=False)
        up = ((me >> bit) & 1) == 1
        keep = jnp.where(up, hi, lo)
        send = jnp.where(up, lo, hi)
        x = keep + lax.ppermute(send, axis, partner(axis, n, bit))
        held.pop(a)
    return x


def split_gather(x, axis):
    orders = GATHER_BITS[axis]
    w = x.shape[1] // len(orders)
    return jnp.concatenate(
        [tree_gather(x[:, i * w:(i + 1) * w], axis, o) for i, o in enumerate(orders)], 1
    )


def split_scatter(x, axis):
    orders = SCATTER_BITS[axis]
    w = x.shape[1] // len(orders)
    return jnp.concatenate(
        [tree_scatter(x[:, i * w:(i + 1) * w], axis, o) for i, o in enumerate(orders)], 1
    )


def row_total(part):
    return tree_sum(part, ROWS)


def col_total(part):
    return tree_sum(part, COLS)


def times_vector(kernel, vector):
    return jnp.sum(kernel.astype(jnp.float32) * vector[None, :], axis=1)


def vector_times(vector, kernel):
    return jnp.sum(vector[:, None] * kernel.astype(jnp.float32), axis=0)


def per_device(src_emb, right_sentence_vectors, src_mass, tgt_mass):
    src_rows = split_gather(src_emb, ROWS)
    target_rows = split_gather(right_sentence_vectors, COLS)
    src_count = src_emb.shape[0]
    tgt_count = right_sentence_vectors.shape[0]
    own_src = lax.dynamic_slice_in_dim(src_mass, lax.axis_index(("y_hi", "x")) * src_count, src_count)
    own_tgt = lax.dynamic_slice_in_dim(
        tgt_mass, lax.axis_index(("y_lo", "z", "core")) * tgt_count, tgt_count
    )
    src_mass = tree_gather(own_src, ROWS, GATHER_BITS[ROWS][0])
    tgt_mass = tree_gather(own_tgt, COLS, GATHER_BITS[COLS][0])

    kernel_grid = (
        lax.dot_general(
            src_rows, target_rows, (((1,), (1,)), ((), ())), preferred_element_type=jnp.float32
        )
        / regularizer_epsilon
    )
    kernel = lax.optimization_barrier(jnp.exp(kernel_grid).astype(jnp.bfloat16))
    weighted = kernel * kernel_grid

    vector = jnp.ones(tgt_mass.shape, jnp.float32)
    old_saved, row_saved, src_saved, col_saved, tgt_saved = ([], [], [], [], [])
    tgt_adj = None
    for iteration in range(ITERS):
        old_saved.append(vector)
        row_sum = row_total(times_vector(kernel, vector))
        src_scale = src_mass / row_sum
        if iteration == ITERS - 1:
            both = col_total(
                jnp.stack([vector_times(src_scale, kernel), vector_times(src_scale, weighted)])
            )
            col_sum, tgt_adj = both[0], both[1]
        else:
            col_sum = col_total(vector_times(src_scale, kernel))
        vector = tgt_mass / col_sum
        row_saved.append(row_sum)
        src_saved.append(src_scale)
        col_saved.append(col_sum)
        tgt_saved.append(vector)
    last_src = src_saved[-1]
    last_tgt = tgt_saved[-1]
    row_bars = [None] * ITERS
    col_bars = [None] * ITERS
    for iteration in reversed(range(ITERS)):
        col_bar = -tgt_adj * tgt_saved[iteration] / col_saved[iteration]
        part = times_vector(kernel, col_bar)
        if iteration == ITERS - 1:
            part = part + times_vector(weighted, last_tgt)
        back = row_total(part)
        row_bar = -back * src_saved[iteration] / row_saved[iteration]
        if iteration > 0:
            tgt_adj = col_total(vector_times(row_bar, kernel))
        row_bars[iteration] = row_bar
        col_bars[iteration] = col_bar
    left = jnp.stack(row_bars + src_saved, axis=1)
    right = jnp.stack(old_saved + col_bars, axis=1)
    lowrank = left[:, 0, None] * right[None, :, 0]
    for k in range(1, left.shape[1]):
        lowrank = lowrank + left[:, k, None] * right[None, :, k]
    cross_term_grid = (
        kernel * (last_src[:, None] * last_tgt[None, :] * (1.0 + kernel_grid) + lowrank)
    ).astype(jnp.bfloat16)
    left_share_piece = (
        jnp.dot(cross_term_grid, target_rows, preferred_element_type=jnp.float32)
        / regularizer_epsilon
    )
    right_share_piece = (
        lax.dot_general(
            cross_term_grid, src_rows, (((0,), (0,)), ((), ())), preferred_element_type=jnp.float32
        )
        / regularizer_epsilon
    )
    grad_src = split_scatter(left_share_piece, ROWS)
    grad_tgt = split_scatter(right_share_piece, COLS)
    return (grad_src, grad_tgt)


def solution(mesh):
    physical = Mesh(mesh.devices.reshape(2, 4, 2, 2, 4), PHYSICAL)
    src_axes = ("y_lo", "z", "core")
    tgt_axes = ("y_hi", "x")
    placed = (
        P(src_axes + tgt_axes, None),
        P(tgt_axes + src_axes, None),
        P(src_axes),
        P(tgt_axes),
    )
    return jax.shard_map(
        per_device,
        mesh=physical,
        in_specs=placed,
        out_specs=(P(src_axes + tgt_axes, None), P(tgt_axes + src_axes, None)),
        check_vma=False,
    )
```

```python
import jax
import jax.numpy as jnp
from jax import lax
from jax.sharding import Mesh, PartitionSpec as P

ITERS = 4


regularizer_epsilon = 0.05
highest = lax.Precision.HIGHEST

PHYSICAL = ("y_lo", "z", "core", "y_hi", "x")
ROWS = ("y_lo", "core", "y_hi")
COLS = ("z", "x")

GATHER_BITS = {ROWS: ((0, 2, 1), (2, 0, 1)), COLS: ((1, 3, 2, 0), (3, 1, 0, 2))}
SCATTER_BITS = {ROWS: ((1, 2, 0), (1, 0, 2)), COLS: ((0, 2, 1, 3), (2, 0, 3, 1))}


def partner(axis, n, bit):
    return [(i, i ^ (1 << bit)) for i in range(n)]


def axis_size(axis):
    return lax.axis_size(axis)


def tree_sum(x, axis):
    n = axis_size(axis)
    spread = jnp.broadcast_to(x[None], (n,) + x.shape)
    return lax.all_to_all(spread, axis, 0, 0, tiled=False).sum(0)


def tree_gather(x, axis, order):
    n = axis_size(axis)
    me = lax.axis_index(axis)
    for bit in order:
        other = lax.ppermute(x, axis, partner(axis, n, bit))
        up = ((me >> bit) & 1) == 1
        x = jnp.where(up, jnp.stack([other, x]), jnp.stack([x, other]))
    held = list(reversed(order))
    perm = [held.index(b) for b in reversed(range(len(order)))]
    x = jnp.transpose(x, perm + list(range(len(order), x.ndim)))
    return x.reshape((n * x.shape[len(order)],) + x.shape[len(order) + 1:])


def tree_scatter(x, axis, order):
    n = axis_size(axis)
    me = lax.axis_index(axis)
    k = len(order)
    rows = x.shape[0] // n
    x = x.reshape((2,) * k + (rows,) + x.shape[1:])
    held = list(reversed(range(k)))
    for bit in order:
        a = held.index(bit)
        lo = lax.index_in_dim(x, 0, a, keepdims=False)
        hi = lax.index_in_dim(x, 1, a, keepdims=False)
        up = ((me >> bit) & 1) == 1
        keep = jnp.where(up, hi, lo)
        send = jnp.where(up, lo, hi)
        x = keep + lax.ppermute(send, axis, partner(axis, n, bit))
        held.pop(a)
    return x


def split_gather(x, axis):
    orders = GATHER_BITS[axis]
    w = x.shape[1] // len(orders)
    return jnp.concatenate(
        [tree_gather(x[:, i * w:(i + 1) * w], axis, o) for i, o in enumerate(orders)], 1
    )


def split_scatter(x, axis):
    orders = SCATTER_BITS[axis]
    w = x.shape[1] // len(orders)
    return jnp.concatenate(
        [tree_scatter(x[:, i * w:(i + 1) * w], axis, o) for i, o in enumerate(orders)], 1
    )


def to_bf16_grid(x):
    return lax.reduce_precision(x, exponent_bits=8, mantissa_bits=7)


def split3(x):
    high = to_bf16_grid(x)
    rest = x - high
    mid = to_bf16_grid(rest)
    low = rest - mid
    return [p.astype(jnp.bfloat16) for p in (high, mid, low)]


EXTRA = 16


def gather_with_mass(rows, mass, axis):
    count, width = rows.shape
    pieces = jnp.concatenate(split3(mass))
    extra = jnp.zeros((EXTRA, width), rows.dtype)
    extra = lax.dynamic_update_slice(extra, pieces[None, :], (0, 0))
    both = split_gather(jnp.concatenate([rows, extra]), axis)
    n = both.shape[0] // (count + EXTRA)
    both = both.reshape(n, count + EXTRA, width)
    got = both[:, count, : 3 * count].astype(jnp.float32).reshape(n, 3, count)
    return both[:, :count].reshape(n * count, width), (got[:, 0] + got[:, 1] + got[:, 2]).reshape(n * count)


def row_total(part):
    return tree_sum(part, ROWS)


def col_total(part):
    return tree_sum(part, COLS)


def times_vector(kernel, vector):
    return jnp.sum(kernel.astype(jnp.float32) * vector[None, :], axis=1)


def vector_times(vector, kernel):
    return jnp.sum(vector[:, None] * kernel.astype(jnp.float32), axis=0)


def per_device(src_emb, right_sentence_vectors, src_mass, tgt_mass):
    src_count = src_emb.shape[0]
    tgt_count = right_sentence_vectors.shape[0]
    own_src = lax.dynamic_slice_in_dim(src_mass, lax.axis_index(("y_hi", "x")) * src_count, src_count)
    own_tgt = lax.dynamic_slice_in_dim(
        tgt_mass, lax.axis_index(("y_lo", "z", "core")) * tgt_count, tgt_count
    )
    src_rows, src_mass = gather_with_mass(src_emb, own_src, ROWS)
    target_rows, tgt_mass = gather_with_mass(right_sentence_vectors, own_tgt, COLS)

    kernel_grid = (
        lax.dot_general(
            src_rows, target_rows, (((1,), (1,)), ((), ())), preferred_element_type=jnp.float32
        )
        / regularizer_epsilon
    )
    kernel = lax.optimization_barrier(jnp.exp(kernel_grid).astype(jnp.bfloat16))
    weighted = kernel * kernel_grid

    vector = jnp.ones(tgt_mass.shape, jnp.float32)
    old_saved, row_saved, src_saved, col_saved, tgt_saved = ([], [], [], [], [])
    tgt_adj = None
    for iteration in range(ITERS):
        old_saved.append(vector)
        row_sum = row_total(times_vector(kernel, vector))
        src_scale = src_mass / row_sum
        if iteration == ITERS - 1:
            both = col_total(
                jnp.stack([vector_times(src_scale, kernel), vector_times(src_scale, weighted)])
            )
            col_sum, tgt_adj = both[0], both[1]
        else:
            col_sum = col_total(vector_times(src_scale, kernel))
        vector = tgt_mass / col_sum
        row_saved.append(row_sum)
        src_saved.append(src_scale)
        col_saved.append(col_sum)
        tgt_saved.append(vector)
    last_src = src_saved[-1]
    last_tgt = tgt_saved[-1]
    row_bars = [None] * ITERS
    col_bars = [None] * ITERS
    for iteration in reversed(range(ITERS)):
        col_bar = -tgt_adj * tgt_saved[iteration] / col_saved[iteration]
        part = times_vector(kernel, col_bar)
        if iteration == ITERS - 1:
            part = part + times_vector(weighted, last_tgt)
        back = row_total(part)
        row_bar = -back * src_saved[iteration] / row_saved[iteration]
        if iteration > 0:
            tgt_adj = col_total(vector_times(row_bar, kernel))
        row_bars[iteration] = row_bar
        col_bars[iteration] = col_bar
    left = jnp.stack(row_bars + src_saved, axis=1)
    right = jnp.stack(old_saved + col_bars, axis=1)
    lowrank = left[:, 0, None] * right[None, :, 0]
    for k in range(1, left.shape[1]):
        lowrank = lowrank + left[:, k, None] * right[None, :, k]
    cross_term_grid = (
        kernel * (last_src[:, None] * last_tgt[None, :] * (1.0 + kernel_grid) + lowrank)
    ).astype(jnp.bfloat16)
    left_share_piece = (
        jnp.dot(cross_term_grid, target_rows, preferred_element_type=jnp.float32)
        / regularizer_epsilon
    )
    right_share_piece = (
        lax.dot_general(
            cross_term_grid, src_rows, (((0,), (0,)), ((), ())), preferred_element_type=jnp.float32
        )
        / regularizer_epsilon
    )
    grad_src = split_scatter(left_share_piece, ROWS)
    grad_tgt = split_scatter(right_share_piece, COLS)
    return (grad_src, grad_tgt)


def solution(mesh):
    physical = Mesh(mesh.devices.reshape(2, 4, 2, 2, 4), PHYSICAL)
    src_axes = ("y_lo", "z", "core")
    tgt_axes = ("y_hi", "x")
    placed = (
        P(src_axes + tgt_axes, None),
        P(tgt_axes + src_axes, None),
        P(src_axes),
        P(tgt_axes),
    )
    return jax.shard_map(
        per_device,
        mesh=physical,
        in_specs=placed,
        out_specs=(P(src_axes + tgt_axes, None), P(tgt_axes + src_axes, None)),
        check_vma=False,
    )
```

```python
import jax
import jax.numpy as jnp
from jax import lax
from jax.sharding import Mesh, PartitionSpec as P

ITERS = 4


regularizer_epsilon = 0.05
highest = lax.Precision.HIGHEST

PHYSICAL = ("y_lo", "z", "core", "y_hi", "x")
ROWS = ("y_lo", "core", "y_hi")
COLS = ("z", "x")

GATHER_BITS = {ROWS: ((0, 2, 1), (2, 0, 1)), COLS: ((1, 3, 2, 0), (3, 1, 0, 2))}
SCATTER_BITS = {ROWS: ((1, 2, 0), (1, 0, 2)), COLS: ((0, 2, 1, 3), (2, 0, 3, 1))}


def partner(axis, n, bit):
    return [(i, i ^ (1 << bit)) for i in range(n)]


def axis_size(axis):
    return lax.axis_size(axis)


def tree_sum(x, axis):
    n = axis_size(axis)
    spread = jnp.broadcast_to(x[None], (n,) + x.shape)
    return lax.all_to_all(spread, axis, 0, 0, tiled=False).sum(0)


def tree_gather(x, axis, order):
    n = axis_size(axis)
    me = lax.axis_index(axis)
    for bit in order:
        other = lax.ppermute(x, axis, partner(axis, n, bit))
        up = ((me >> bit) & 1) == 1
        x = jnp.where(up, jnp.stack([other, x]), jnp.stack([x, other]))
    held = list(reversed(order))
    perm = [held.index(b) for b in reversed(range(len(order)))]
    x = jnp.transpose(x, perm + list(range(len(order), x.ndim)))
    return x.reshape((n * x.shape[len(order)],) + x.shape[len(order) + 1:])


def tree_scatter(x, axis, order):
    n = axis_size(axis)
    me = lax.axis_index(axis)
    k = len(order)
    rows = x.shape[0] // n
    x = x.reshape((2,) * k + (rows,) + x.shape[1:])
    held = list(reversed(range(k)))
    for bit in order:
        a = held.index(bit)
        lo = lax.index_in_dim(x, 0, a, keepdims=False)
        hi = lax.index_in_dim(x, 1, a, keepdims=False)
        up = ((me >> bit) & 1) == 1
        keep = jnp.where(up, hi, lo)
        send = jnp.where(up, lo, hi)
        x = keep + lax.ppermute(send, axis, partner(axis, n, bit))
        held.pop(a)
    return x


def column_parts(width, axis):
    if axis == COLS:
        return ((0, 2 * width // 3), (2 * width // 3, width))
    return ((0, width // 2), (width // 2, width))


def split_gather(x, axis):
    parts = column_parts(x.shape[1], axis)
    return jnp.concatenate(
        [tree_gather(x[:, a:b], axis, o) for (a, b), o in zip(parts, GATHER_BITS[axis])], 1
    )


def split_scatter(x, axis):
    parts = column_parts(x.shape[1], axis)
    return jnp.concatenate(
        [tree_scatter(x[:, a:b], axis, o) for (a, b), o in zip(parts, SCATTER_BITS[axis])], 1
    )


def to_bf16_grid(x):
    return lax.reduce_precision(x, exponent_bits=8, mantissa_bits=7)


def split3(x):
    high = to_bf16_grid(x)
    rest = x - high
    mid = to_bf16_grid(rest)
    low = rest - mid
    return [p.astype(jnp.bfloat16) for p in (high, mid, low)]


EXTRA = 16


def gather_with_mass(rows, mass, axis):
    count, width = rows.shape
    pieces = jnp.concatenate(split3(mass))
    extra = jnp.zeros((EXTRA, width), rows.dtype)
    extra = lax.dynamic_update_slice(extra, pieces[None, :], (0, 0))
    both = split_gather(jnp.concatenate([rows, extra]), axis)
    n = both.shape[0] // (count + EXTRA)
    both = both.reshape(n, count + EXTRA, width)
    got = both[:, count, : 3 * count].astype(jnp.float32).reshape(n, 3, count)
    return both[:, :count].reshape(n * count, width), (got[:, 0] + got[:, 1] + got[:, 2]).reshape(n * count)


def row_total(part):
    return tree_sum(part, ROWS)


def col_total(part):
    return tree_sum(part, COLS)


def times_vector(kernel, vector):
    return jnp.sum(kernel.astype(jnp.float32) * vector[None, :], axis=1)


def vector_times(vector, kernel):
    return jnp.sum(vector[:, None] * kernel.astype(jnp.float32), axis=0)


def per_device(src_emb, right_sentence_vectors, src_mass, tgt_mass):
    src_count = src_emb.shape[0]
    tgt_count = right_sentence_vectors.shape[0]
    own_src = lax.dynamic_slice_in_dim(src_mass, lax.axis_index(("y_hi", "x")) * src_count, src_count)
    own_tgt = lax.dynamic_slice_in_dim(
        tgt_mass, lax.axis_index(("y_lo", "z", "core")) * tgt_count, tgt_count
    )
    src_rows, src_mass = gather_with_mass(src_emb, own_src, ROWS)
    target_rows, tgt_mass = gather_with_mass(right_sentence_vectors, own_tgt, COLS)

    kernel_grid = (
        lax.dot_general(
            src_rows, target_rows, (((1,), (1,)), ((), ())), preferred_element_type=jnp.float32
        )
        / regularizer_epsilon
    )
    kernel = lax.optimization_barrier(jnp.exp(kernel_grid).astype(jnp.bfloat16))
    weighted = kernel * kernel_grid

    vector = jnp.ones(tgt_mass.shape, jnp.float32)
    old_saved, row_saved, src_saved, col_saved, tgt_saved = ([], [], [], [], [])
    tgt_adj = None
    for iteration in range(ITERS):
        old_saved.append(vector)
        row_sum = row_total(times_vector(kernel, vector))
        src_scale = src_mass / row_sum
        if iteration == ITERS - 1:
            both = col_total(
                jnp.stack([vector_times(src_scale, kernel), vector_times(src_scale, weighted)])
            )
            col_sum, tgt_adj = both[0], both[1]
        else:
            col_sum = col_total(vector_times(src_scale, kernel))
        vector = tgt_mass / col_sum
        row_saved.append(row_sum)
        src_saved.append(src_scale)
        col_saved.append(col_sum)
        tgt_saved.append(vector)
    last_src = src_saved[-1]
    last_tgt = tgt_saved[-1]
    row_bars = [None] * ITERS
    col_bars = [None] * ITERS
    for iteration in reversed(range(ITERS)):
        col_bar = -tgt_adj * tgt_saved[iteration] / col_saved[iteration]
        part = times_vector(kernel, col_bar)
        if iteration == ITERS - 1:
            part = part + times_vector(weighted, last_tgt)
        back = row_total(part)
        row_bar = -back * src_saved[iteration] / row_saved[iteration]
        if iteration > 0:
            tgt_adj = col_total(vector_times(row_bar, kernel))
        row_bars[iteration] = row_bar
        col_bars[iteration] = col_bar
    left = jnp.stack(row_bars + src_saved, axis=1)
    right = jnp.stack(old_saved + col_bars, axis=1)
    lowrank = left[:, 0, None] * right[None, :, 0]
    for k in range(1, left.shape[1]):
        lowrank = lowrank + left[:, k, None] * right[None, :, k]
    cross_term_grid = (
        kernel * (last_src[:, None] * last_tgt[None, :] * (1.0 + kernel_grid) + lowrank)
    ).astype(jnp.bfloat16)
    left_share_piece = (
        jnp.dot(cross_term_grid, target_rows, preferred_element_type=jnp.float32)
        / regularizer_epsilon
    )
    right_share_piece = (
        lax.dot_general(
            cross_term_grid, src_rows, (((0,), (0,)), ((), ())), preferred_element_type=jnp.float32
        )
        / regularizer_epsilon
    )
    grad_src = split_scatter(left_share_piece, ROWS)
    grad_tgt = split_scatter(right_share_piece, COLS)
    return (grad_src, grad_tgt)


def solution(mesh):
    physical = Mesh(mesh.devices.reshape(2, 4, 2, 2, 4), PHYSICAL)
    src_axes = ("y_lo", "z", "core")
    tgt_axes = ("y_hi", "x")
    placed = (
        P(src_axes + tgt_axes, None),
        P(tgt_axes + src_axes, None),
        P(src_axes),
        P(tgt_axes),
    )
    return jax.shard_map(
        per_device,
        mesh=physical,
        in_specs=placed,
        out_specs=(P(src_axes + tgt_axes, None), P(tgt_axes + src_axes, None)),
        check_vma=False,
    )
```

```python
import jax
import jax.numpy as jnp
from jax import lax
from jax.sharding import Mesh, PartitionSpec as P

ITERS = 4


regularizer_epsilon = 0.05
highest = lax.Precision.HIGHEST

PHYSICAL = ("y_lo", "z", "core", "y_hi", "x")
ROWS = ("y_lo", "core", "y_hi")
COLS = ("z", "x")

GATHER_BITS = {ROWS: ((0, 2, 1), (2, 0, 1)), COLS: ((1, 3, 2, 0), (3, 1, 0, 2))}
SCATTER_BITS = {ROWS: ((1, 2, 0), (1, 0, 2)), COLS: ((0, 2, 1, 3), (2, 0, 3, 1))}


def partner(axis, n, bit):
    return [(i, i ^ (1 << bit)) for i in range(n)]


def axis_size(axis):
    return lax.axis_size(axis)


def tree_sum(x, axis):
    n = axis_size(axis)
    spread = jnp.broadcast_to(x[None], (n,) + x.shape)
    return lax.all_to_all(spread, axis, 0, 0, tiled=False).sum(0)


def tree_gather(x, axis, order):
    n = axis_size(axis)
    me = lax.axis_index(axis)
    for bit in order:
        other = lax.ppermute(x, axis, partner(axis, n, bit))
        up = ((me >> bit) & 1) == 1
        x = jnp.where(up, jnp.stack([other, x]), jnp.stack([x, other]))
    held = list(reversed(order))
    perm = [held.index(b) for b in reversed(range(len(order)))]
    x = jnp.transpose(x, perm + list(range(len(order), x.ndim)))
    return x.reshape((n * x.shape[len(order)],) + x.shape[len(order) + 1:])


def tree_scatter(x, axis, order):
    n = axis_size(axis)
    me = lax.axis_index(axis)
    k = len(order)
    rows = x.shape[0] // n
    x = x.reshape((2,) * k + (rows,) + x.shape[1:])
    held = list(reversed(range(k)))
    for bit in order:
        a = held.index(bit)
        lo = lax.index_in_dim(x, 0, a, keepdims=False)
        hi = lax.index_in_dim(x, 1, a, keepdims=False)
        up = ((me >> bit) & 1) == 1
        keep = jnp.where(up, hi, lo)
        send = jnp.where(up, lo, hi)
        x = keep + lax.ppermute(send, axis, partner(axis, n, bit))
        held.pop(a)
    return x


def split_gather(x, axis):
    orders = GATHER_BITS[axis]
    w = x.shape[1] // len(orders)
    return jnp.concatenate(
        [tree_gather(x[:, i * w:(i + 1) * w], axis, o) for i, o in enumerate(orders)], 1
    )


def split_scatter(x, axis):
    orders = SCATTER_BITS[axis]
    w = x.shape[1] // len(orders)
    return jnp.concatenate(
        [tree_scatter(x[:, i * w:(i + 1) * w], axis, o) for i, o in enumerate(orders)], 1
    )


def to_bf16_grid(x):
    return lax.reduce_precision(x, exponent_bits=8, mantissa_bits=7)


def split3(x):
    high = to_bf16_grid(x)
    rest = x - high
    mid = to_bf16_grid(rest)
    low = rest - mid
    return [p.astype(jnp.bfloat16) for p in (high, mid, low)]


EXTRA = 16


def gather_with_mass(rows, mass, axis):
    count, width = rows.shape
    pieces = jnp.concatenate(split3(mass))
    extra = jnp.zeros((EXTRA, width), rows.dtype)
    extra = lax.dynamic_update_slice(extra, pieces[None, :], (0, 0))
    both = split_gather(jnp.concatenate([rows, extra]), axis)
    n = both.shape[0] // (count + EXTRA)
    both = both.reshape(n, count + EXTRA, width)
    got = both[:, count, : 3 * count].astype(jnp.float32).reshape(n, 3, count)
    return both[:, :count].reshape(n * count, width), (got[:, 0] + got[:, 1] + got[:, 2]).reshape(n * count)


def row_total(part):
    return tree_sum(part, ROWS)


def col_total(part):
    return tree_sum(part, COLS)


def times_vector(kernel, vector):
    return jnp.sum(kernel.astype(jnp.float32) * vector[None, :], axis=1)


def vector_times(vector, kernel):
    return jnp.sum(vector[:, None] * kernel.astype(jnp.float32), axis=0)


def per_device(src_emb, right_sentence_vectors, src_mass, tgt_mass):
    src_count = src_emb.shape[0]
    tgt_count = right_sentence_vectors.shape[0]
    own_src = lax.dynamic_slice_in_dim(src_mass, lax.axis_index(("y_hi", "x")) * src_count, src_count)
    own_tgt = lax.dynamic_slice_in_dim(
        tgt_mass, lax.axis_index(("y_lo", "z", "core")) * tgt_count, tgt_count
    )
    src_rows, src_mass = gather_with_mass(src_emb, own_src, ROWS)
    target_rows, tgt_mass = gather_with_mass(right_sentence_vectors, own_tgt, COLS)

    kernel_grid = (
        lax.dot_general(
            src_rows, target_rows, (((1,), (1,)), ((), ())), preferred_element_type=jnp.float32
        )
        / regularizer_epsilon
    )
    kernel = lax.optimization_barrier(jnp.exp(kernel_grid).astype(jnp.bfloat16))
    weighted = kernel * kernel_grid

    vector = jnp.ones(tgt_mass.shape, jnp.float32)
    old_saved, row_saved, src_saved, col_saved, tgt_saved = ([], [], [], [], [])
    tgt_adj = None
    for iteration in range(ITERS):
        old_saved.append(vector)
        row_sum = row_total(times_vector(kernel, vector))
        src_scale = src_mass / row_sum
        if iteration == ITERS - 1:
            both = col_total(
                jnp.stack([vector_times(src_scale, kernel), vector_times(src_scale, weighted)])
            )
            col_sum, tgt_adj = both[0], both[1]
        else:
            col_sum = col_total(vector_times(src_scale, kernel))
        vector = tgt_mass / col_sum
        row_saved.append(row_sum)
        src_saved.append(src_scale)
        col_saved.append(col_sum)
        tgt_saved.append(vector)
    last_src = src_saved[-1]
    last_tgt = tgt_saved[-1]
    row_bars = [None] * ITERS
    col_bars = [None] * ITERS
    for iteration in reversed(range(ITERS)):
        col_bar = -tgt_adj * tgt_saved[iteration] / col_saved[iteration]
        part = times_vector(kernel, col_bar)
        if iteration == ITERS - 1:
            part = part + times_vector(weighted, last_tgt)
        back = row_total(part)
        row_bar = -back * src_saved[iteration] / row_saved[iteration]
        if iteration > 0:
            tgt_adj = col_total(vector_times(row_bar, kernel))
        row_bars[iteration] = row_bar
        col_bars[iteration] = col_bar
    left = jnp.stack(row_bars + src_saved, axis=1)
    right = jnp.stack(old_saved + col_bars, axis=1)
    left_pieces, right_pieces = split3(left), split3(right)
    left_all = jnp.concatenate([a for a in left_pieces for b in right_pieces], axis=1)
    right_all = jnp.concatenate([b for a in left_pieces for b in right_pieces], axis=1)
    lowrank = lax.dot_general(
        left_all, right_all, (((1,), (1,)), ((), ())), preferred_element_type=jnp.float32
    )
    cross_term_grid = (
        kernel * (last_src[:, None] * last_tgt[None, :] * (1.0 + kernel_grid) + lowrank)
    ).astype(jnp.bfloat16)
    left_share_piece = (
        jnp.dot(cross_term_grid, target_rows, preferred_element_type=jnp.float32)
        / regularizer_epsilon
    )
    right_share_piece = (
        lax.dot_general(
            cross_term_grid, src_rows, (((0,), (0,)), ((), ())), preferred_element_type=jnp.float32
        )
        / regularizer_epsilon
    )
    grad_src = split_scatter(left_share_piece, ROWS)
    grad_tgt = split_scatter(right_share_piece, COLS)
    return (grad_src, grad_tgt)


def solution(mesh):
    physical = Mesh(mesh.devices.reshape(2, 4, 2, 2, 4), PHYSICAL)
    src_axes = ("y_lo", "z", "core")
    tgt_axes = ("y_hi", "x")
    placed = (
        P(src_axes + tgt_axes, None),
        P(tgt_axes + src_axes, None),
        P(src_axes),
        P(tgt_axes),
    )
    return jax.shard_map(
        per_device,
        mesh=physical,
        in_specs=placed,
        out_specs=(P(src_axes + tgt_axes, None), P(tgt_axes + src_axes, None)),
        check_vma=False,
    )
```

```python
import jax
import jax.numpy as jnp
from jax import lax
from jax.sharding import Mesh, PartitionSpec as P

ITERS = 4


regularizer_epsilon = 0.05
highest = lax.Precision.HIGHEST

PHYSICAL = ("y_lo", "z", "core", "y_hi", "x")
ROWS = ("y_lo", "core", "y_hi")
COLS = ("z", "x")

GATHER_BITS = {ROWS: ((0, 2, 1), (2, 0, 1)), COLS: ((1, 3, 2, 0), (3, 1, 0, 2))}
SCATTER_BITS = {ROWS: ((1, 2, 0), (1, 0, 2)), COLS: ((0, 2, 1, 3), (2, 0, 3, 1))}


def partner(axis, n, bit):
    return [(i, i ^ (1 << bit)) for i in range(n)]


def axis_size(axis):
    return lax.axis_size(axis)


def tree_sum(x, axis):
    n = axis_size(axis)
    spread = jnp.broadcast_to(x[None], (n,) + x.shape)
    return lax.all_to_all(spread, axis, 0, 0, tiled=False).sum(0)


def tree_gather(x, axis, order):
    n = axis_size(axis)
    me = lax.axis_index(axis)
    for bit in order:
        other = lax.ppermute(x, axis, partner(axis, n, bit))
        up = ((me >> bit) & 1) == 1
        x = jnp.where(up, jnp.stack([other, x]), jnp.stack([x, other]))
    held = list(reversed(order))
    perm = [held.index(b) for b in reversed(range(len(order)))]
    x = jnp.transpose(x, perm + list(range(len(order), x.ndim)))
    return x.reshape((n * x.shape[len(order)],) + x.shape[len(order) + 1:])


def tree_scatter(x, axis, order):
    n = axis_size(axis)
    me = lax.axis_index(axis)
    k = len(order)
    rows = x.shape[0] // n
    x = x.reshape((2,) * k + (rows,) + x.shape[1:])
    held = list(reversed(range(k)))
    for bit in order:
        a = held.index(bit)
        lo = lax.index_in_dim(x, 0, a, keepdims=False)
        hi = lax.index_in_dim(x, 1, a, keepdims=False)
        up = ((me >> bit) & 1) == 1
        keep = jnp.where(up, hi, lo)
        send = jnp.where(up, lo, hi)
        x = keep + lax.ppermute(send, axis, partner(axis, n, bit))
        held.pop(a)
    return x


def column_parts(width, axis):
    if axis == COLS:
        return ((0, width // 3), (width // 3, width))
    return ((0, width // 2), (width // 2, width))


def split_gather(x, axis):
    parts = column_parts(x.shape[1], axis)
    return jnp.concatenate(
        [tree_gather(x[:, a:b], axis, o) for (a, b), o in zip(parts, GATHER_BITS[axis])], 1
    )


def split_scatter(x, axis):
    parts = column_parts(x.shape[1], axis)
    return jnp.concatenate(
        [tree_scatter(x[:, a:b], axis, o) for (a, b), o in zip(parts, SCATTER_BITS[axis])], 1
    )


def to_bf16_grid(x):
    return lax.reduce_precision(x, exponent_bits=8, mantissa_bits=7)


def split3(x):
    high = to_bf16_grid(x)
    rest = x - high
    mid = to_bf16_grid(rest)
    low = rest - mid
    return [p.astype(jnp.bfloat16) for p in (high, mid, low)]


EXTRA = 16


def gather_with_mass(rows, mass, axis):
    count, width = rows.shape
    pieces = jnp.concatenate(split3(mass))
    extra = jnp.zeros((EXTRA, width), rows.dtype)
    extra = lax.dynamic_update_slice(extra, pieces[None, :], (0, 0))
    both = split_gather(jnp.concatenate([rows, extra]), axis)
    n = both.shape[0] // (count + EXTRA)
    both = both.reshape(n, count + EXTRA, width)
    got = both[:, count, : 3 * count].astype(jnp.float32).reshape(n, 3, count)
    return both[:, :count].reshape(n * count, width), (got[:, 0] + got[:, 1] + got[:, 2]).reshape(n * count)


def row_total(part):
    return tree_sum(part, ROWS)


def col_total(part):
    return tree_sum(part, COLS)


def times_vector(kernel, vector):
    return jnp.sum(kernel.astype(jnp.float32) * vector[None, :], axis=1)


def vector_times(vector, kernel):
    return jnp.sum(vector[:, None] * kernel.astype(jnp.float32), axis=0)


def per_device(src_emb, right_sentence_vectors, src_mass, tgt_mass):
    src_count = src_emb.shape[0]
    tgt_count = right_sentence_vectors.shape[0]
    own_src = lax.dynamic_slice_in_dim(src_mass, lax.axis_index(("y_hi", "x")) * src_count, src_count)
    own_tgt = lax.dynamic_slice_in_dim(
        tgt_mass, lax.axis_index(("y_lo", "z", "core")) * tgt_count, tgt_count
    )
    src_rows, src_mass = gather_with_mass(src_emb, own_src, ROWS)
    target_rows, tgt_mass = gather_with_mass(right_sentence_vectors, own_tgt, COLS)

    kernel_grid = (
        lax.dot_general(
            src_rows, target_rows, (((1,), (1,)), ((), ())), preferred_element_type=jnp.float32
        )
        / regularizer_epsilon
    )
    kernel = lax.optimization_barrier(jnp.exp(kernel_grid).astype(jnp.bfloat16))
    weighted = kernel * kernel_grid

    vector = jnp.ones(tgt_mass.shape, jnp.float32)
    old_saved, row_saved, src_saved, col_saved, tgt_saved = ([], [], [], [], [])
    tgt_adj = None
    for iteration in range(ITERS):
        old_saved.append(vector)
        row_sum = row_total(times_vector(kernel, vector))
        src_scale = src_mass / row_sum
        if iteration == ITERS - 1:
            both = col_total(
                jnp.stack([vector_times(src_scale, kernel), vector_times(src_scale, weighted)])
            )
            col_sum, tgt_adj = both[0], both[1]
        else:
            col_sum = col_total(vector_times(src_scale, kernel))
        vector = tgt_mass / col_sum
        row_saved.append(row_sum)
        src_saved.append(src_scale)
        col_saved.append(col_sum)
        tgt_saved.append(vector)
    last_src = src_saved[-1]
    last_tgt = tgt_saved[-1]
    row_bars = [None] * ITERS
    col_bars = [None] * ITERS
    for iteration in reversed(range(ITERS)):
        col_bar = -tgt_adj * tgt_saved[iteration] / col_saved[iteration]
        part = times_vector(kernel, col_bar)
        if iteration == ITERS - 1:
            part = part + times_vector(weighted, last_tgt)
        back = row_total(part)
        row_bar = -back * src_saved[iteration] / row_saved[iteration]
        if iteration > 0:
            tgt_adj = col_total(vector_times(row_bar, kernel))
        row_bars[iteration] = row_bar
        col_bars[iteration] = col_bar
    left = jnp.stack(row_bars + src_saved, axis=1)
    right = jnp.stack(old_saved + col_bars, axis=1)
    lowrank = left[:, 0, None] * right[None, :, 0]
    for k in range(1, left.shape[1]):
        lowrank = lowrank + left[:, k, None] * right[None, :, k]
    cross_term_grid = (
        kernel * (last_src[:, None] * last_tgt[None, :] * (1.0 + kernel_grid) + lowrank)
    ).astype(jnp.bfloat16)
    left_share_piece = (
        jnp.dot(cross_term_grid, target_rows, preferred_element_type=jnp.float32)
        / regularizer_epsilon
    )
    right_share_piece = (
        lax.dot_general(
            cross_term_grid, src_rows, (((0,), (0,)), ((), ())), preferred_element_type=jnp.float32
        )
        / regularizer_epsilon
    )
    grad_src = split_scatter(left_share_piece, ROWS)
    grad_tgt = split_scatter(right_share_piece, COLS)
    return (grad_src, grad_tgt)


def solution(mesh):
    physical = Mesh(mesh.devices.reshape(2, 4, 2, 2, 4), PHYSICAL)
    src_axes = ("y_lo", "z", "core")
    tgt_axes = ("y_hi", "x")
    placed = (
        P(src_axes + tgt_axes, None),
        P(tgt_axes + src_axes, None),
        P(src_axes),
        P(tgt_axes),
    )
    return jax.shard_map(
        per_device,
        mesh=physical,
        in_specs=placed,
        out_specs=(P(src_axes + tgt_axes, None), P(tgt_axes + src_axes, None)),
        check_vma=False,
    )
```

```python
import jax
import jax.numpy as jnp
from jax import lax
from jax.sharding import Mesh, PartitionSpec as P

ITERS = 4


regularizer_epsilon = 0.05
highest = lax.Precision.HIGHEST

PHYSICAL = ("y_lo", "z", "core", "y_hi", "x")
ROWS = ("y_lo", "core", "y_hi")
COLS = ("z", "x")

GATHER_BITS = {ROWS: ((0, 2, 1), (2, 0, 1)), COLS: ((1, 3, 2, 0), (3, 1, 0, 2))}
SCATTER_BITS = {ROWS: ((1, 2, 0), (1, 0, 2)), COLS: ((0, 2, 1, 3), (2, 0, 3, 1))}


def partner(axis, n, bit):
    return [(i, i ^ (1 << bit)) for i in range(n)]


def axis_size(axis):
    return lax.axis_size(axis)


def tree_sum(x, axis):
    n = axis_size(axis)
    spread = jnp.broadcast_to(x[None], (n,) + x.shape)
    return lax.all_to_all(spread, axis, 0, 0, tiled=False).sum(0)


def tree_gather(x, axis, order):
    n = axis_size(axis)
    me = lax.axis_index(axis)
    for bit in order:
        other = lax.ppermute(x, axis, partner(axis, n, bit))
        up = ((me >> bit) & 1) == 1
        x = jnp.where(up, jnp.stack([other, x]), jnp.stack([x, other]))
    held = list(reversed(order))
    perm = [held.index(b) for b in reversed(range(len(order)))]
    x = jnp.transpose(x, perm + list(range(len(order), x.ndim)))
    return x.reshape((n * x.shape[len(order)],) + x.shape[len(order) + 1:])


def tree_scatter(x, axis, order):
    n = axis_size(axis)
    me = lax.axis_index(axis)
    k = len(order)
    rows = x.shape[0] // n
    x = x.reshape((2,) * k + (rows,) + x.shape[1:])
    held = list(reversed(range(k)))
    for bit in order:
        a = held.index(bit)
        lo = lax.index_in_dim(x, 0, a, keepdims=False)
        hi = lax.index_in_dim(x, 1, a, keepdims=False)
        up = ((me >> bit) & 1) == 1
        keep = jnp.where(up, hi, lo)
        send = jnp.where(up, lo, hi)
        x = keep + lax.ppermute(send, axis, partner(axis, n, bit))
        held.pop(a)
    return x


def split_gather(x, axis):
    orders = GATHER_BITS[axis]
    w = x.shape[1] // len(orders)
    return jnp.concatenate(
        [tree_gather(x[:, i * w:(i + 1) * w], axis, o) for i, o in enumerate(orders)], 1
    )


def split_scatter(x, axis):
    orders = SCATTER_BITS[axis]
    w = x.shape[1] // len(orders)
    return jnp.concatenate(
        [tree_scatter(x[:, i * w:(i + 1) * w], axis, o) for i, o in enumerate(orders)], 1
    )


def to_bf16_grid(x):
    return lax.reduce_precision(x, exponent_bits=8, mantissa_bits=7)


def split3(x):
    high = to_bf16_grid(x)
    rest = x - high
    mid = to_bf16_grid(rest)
    low = rest - mid
    return [p.astype(jnp.bfloat16) for p in (high, mid, low)]


EXTRA = 16


def gather_with_mass(rows, mass, axis):
    count, width = rows.shape
    pieces = jnp.concatenate(split3(mass))
    extra = jnp.zeros((EXTRA, width), rows.dtype)
    extra = lax.dynamic_update_slice(extra, pieces[None, :], (0, 0))
    both = split_gather(jnp.concatenate([rows, extra]), axis)
    n = both.shape[0] // (count + EXTRA)
    both = both.reshape(n, count + EXTRA, width)
    got = both[:, count, : 3 * count].astype(jnp.float32).reshape(n, 3, count)
    return both[:, :count].reshape(n * count, width), (got[:, 0] + got[:, 1] + got[:, 2]).reshape(n * count)


def sum_and_gather(x, own, axis):
    n = axis_size(axis)
    count = own.shape[0]
    padded = jnp.concatenate([own, jnp.zeros((x.shape[0] - count,), own.dtype)])
    spread = jnp.broadcast_to(jnp.stack([x, padded])[None], (n, 2) + x.shape)
    got = lax.all_to_all(spread, axis, 0, 0, tiled=False)
    return got[:, 0].sum(0), got[:, 1, :count].reshape(n * count)


def row_total(part):
    return tree_sum(part, ROWS)


def col_total(part):
    return tree_sum(part, COLS)


def times_vector(kernel, vector):
    return jnp.sum(kernel.astype(jnp.float32) * vector[None, :], axis=1)


def vector_times(vector, kernel):
    return jnp.sum(vector[:, None] * kernel.astype(jnp.float32), axis=0)


def per_device(src_emb, right_sentence_vectors, src_mass, tgt_mass):
    src_count = src_emb.shape[0]
    tgt_count = right_sentence_vectors.shape[0]
    own_src = lax.dynamic_slice_in_dim(src_mass, lax.axis_index(("y_hi", "x")) * src_count, src_count)
    own_tgt = lax.dynamic_slice_in_dim(
        tgt_mass, lax.axis_index(("y_lo", "z", "core")) * tgt_count, tgt_count
    )
    src_rows = split_gather(src_emb, ROWS)
    target_rows = split_gather(right_sentence_vectors, COLS)

    kernel_grid = (
        lax.dot_general(
            src_rows, target_rows, (((1,), (1,)), ((), ())), preferred_element_type=jnp.float32
        )
        / regularizer_epsilon
    )
    kernel = lax.optimization_barrier(jnp.exp(kernel_grid).astype(jnp.bfloat16))
    weighted = kernel * kernel_grid

    vector = jnp.ones((target_rows.shape[0],), jnp.float32)
    old_saved, row_saved, src_saved, col_saved, tgt_saved = ([], [], [], [], [])
    tgt_adj = None
    for iteration in range(ITERS):
        old_saved.append(vector)
        if iteration == 0:
            row_sum, src_mass = sum_and_gather(times_vector(kernel, vector), own_src, ROWS)
        else:
            row_sum = row_total(times_vector(kernel, vector))
        src_scale = src_mass / row_sum
        if iteration == ITERS - 1:
            both = col_total(
                jnp.stack([vector_times(src_scale, kernel), vector_times(src_scale, weighted)])
            )
            col_sum, tgt_adj = both[0], both[1]
        elif iteration == 0:
            col_sum, tgt_mass = sum_and_gather(vector_times(src_scale, kernel), own_tgt, COLS)
        else:
            col_sum = col_total(vector_times(src_scale, kernel))
        vector = tgt_mass / col_sum
        row_saved.append(row_sum)
        src_saved.append(src_scale)
        col_saved.append(col_sum)
        tgt_saved.append(vector)
    last_src = src_saved[-1]
    last_tgt = tgt_saved[-1]
    row_bars = [None] * ITERS
    col_bars = [None] * ITERS
    for iteration in reversed(range(ITERS)):
        col_bar = -tgt_adj * tgt_saved[iteration] / col_saved[iteration]
        part = times_vector(kernel, col_bar)
        if iteration == ITERS - 1:
            part = part + times_vector(weighted, last_tgt)
        back = row_total(part)
        row_bar = -back * src_saved[iteration] / row_saved[iteration]
        if iteration > 0:
            tgt_adj = col_total(vector_times(row_bar, kernel))
        row_bars[iteration] = row_bar
        col_bars[iteration] = col_bar
    left = jnp.stack(row_bars + src_saved, axis=1)
    right = jnp.stack(old_saved + col_bars, axis=1)
    lowrank = left[:, 0, None] * right[None, :, 0]
    for k in range(1, left.shape[1]):
        lowrank = lowrank + left[:, k, None] * right[None, :, k]
    cross_term_grid = (
        kernel * (last_src[:, None] * last_tgt[None, :] * (1.0 + kernel_grid) + lowrank)
    ).astype(jnp.bfloat16)
    left_share_piece = (
        jnp.dot(cross_term_grid, target_rows, preferred_element_type=jnp.float32)
        / regularizer_epsilon
    )
    right_share_piece = (
        lax.dot_general(
            cross_term_grid, src_rows, (((0,), (0,)), ((), ())), preferred_element_type=jnp.float32
        )
        / regularizer_epsilon
    )
    grad_src = split_scatter(left_share_piece, ROWS)
    grad_tgt = split_scatter(right_share_piece, COLS)
    return (grad_src, grad_tgt)


def solution(mesh):
    physical = Mesh(mesh.devices.reshape(2, 4, 2, 2, 4), PHYSICAL)
    src_axes = ("y_lo", "z", "core")
    tgt_axes = ("y_hi", "x")
    placed = (
        P(src_axes + tgt_axes, None),
        P(tgt_axes + src_axes, None),
        P(src_axes),
        P(tgt_axes),
    )
    return jax.shard_map(
        per_device,
        mesh=physical,
        in_specs=placed,
        out_specs=(P(src_axes + tgt_axes, None), P(tgt_axes + src_axes, None)),
        check_vma=False,
    )
```

```python
import jax
import jax.numpy as jnp
from jax import lax
from jax.sharding import Mesh, PartitionSpec as P

ITERS = 4


regularizer_epsilon = 0.05
highest = lax.Precision.HIGHEST

PHYSICAL = ("y_lo", "z", "core", "y_hi", "x")
ROWS = ("y_lo", "core", "y_hi")
COLS = ("z", "x")

GATHER_BITS = {ROWS: ((0, 2, 1), (2, 0, 1)), COLS: ((1, 3, 2, 0), (3, 1, 0, 2))}
SCATTER_BITS = {ROWS: ((1, 2, 0), (1, 0, 2)), COLS: ((0, 2, 1, 3), (2, 0, 3, 1))}


def partner(axis, n, bit):
    return [(i, i ^ (1 << bit)) for i in range(n)]


def axis_size(axis):
    return lax.axis_size(axis)


def tree_sum(x, axis):
    n = axis_size(axis)
    spread = jnp.broadcast_to(x[None], (n,) + x.shape)
    return lax.all_to_all(spread, axis, 0, 0, tiled=False).sum(0)


def tree_gather(x, axis, order):
    n = axis_size(axis)
    me = lax.axis_index(axis)
    for bit in order:
        other = lax.ppermute(x, axis, partner(axis, n, bit))
        up = ((me >> bit) & 1) == 1
        x = jnp.where(up, jnp.stack([other, x]), jnp.stack([x, other]))
    held = list(reversed(order))
    perm = [held.index(b) for b in reversed(range(len(order)))]
    x = jnp.transpose(x, perm + list(range(len(order), x.ndim)))
    return x.reshape((n * x.shape[len(order)],) + x.shape[len(order) + 1:])


def tree_scatter(x, axis, order):
    n = axis_size(axis)
    me = lax.axis_index(axis)
    k = len(order)
    rows = x.shape[0] // n
    x = x.reshape((2,) * k + (rows,) + x.shape[1:])
    held = list(reversed(range(k)))
    for bit in order:
        a = held.index(bit)
        lo = lax.index_in_dim(x, 0, a, keepdims=False)
        hi = lax.index_in_dim(x, 1, a, keepdims=False)
        up = ((me >> bit) & 1) == 1
        keep = jnp.where(up, hi, lo)
        send = jnp.where(up, lo, hi)
        x = keep + lax.ppermute(send, axis, partner(axis, n, bit))
        held.pop(a)
    return x


def split_gather(x, axis):
    orders = GATHER_BITS[axis]
    w = x.shape[1] // len(orders)
    return jnp.concatenate(
        [tree_gather(x[:, i * w:(i + 1) * w], axis, o) for i, o in enumerate(orders)], 1
    )


def split_scatter(x, axis):
    orders = SCATTER_BITS[axis]
    w = x.shape[1] // len(orders)
    return jnp.concatenate(
        [tree_scatter(x[:, i * w:(i + 1) * w], axis, o) for i, o in enumerate(orders)], 1
    )


def to_bf16_grid(x):
    return lax.reduce_precision(x, exponent_bits=8, mantissa_bits=7)


def split3(x):
    high = to_bf16_grid(x)
    rest = x - high
    mid = to_bf16_grid(rest)
    low = rest - mid
    return [p.astype(jnp.bfloat16) for p in (high, mid, low)]


def sum_and_gather(x, own, axis):
    n = axis_size(axis)
    count = own.shape[0]
    padded = jnp.concatenate([own, jnp.zeros((x.shape[0] - count,), own.dtype)])
    spread = jnp.broadcast_to(jnp.stack([x, padded])[None], (n, 2) + x.shape)
    got = lax.all_to_all(spread, axis, 0, 0, tiled=False)
    return got[:, 0].sum(0), got[:, 1, :count].reshape(n * count)


def row_total(part):
    return tree_sum(part, ROWS)


def col_total(part):
    return tree_sum(part, COLS)


def times_vector(kernel, vector):
    return jnp.sum(kernel.astype(jnp.float32) * vector[None, :], axis=1)


def vector_times(vector, kernel):
    return jnp.sum(vector[:, None] * kernel.astype(jnp.float32), axis=0)


def per_device(src_emb, right_sentence_vectors, src_mass, tgt_mass):
    src_count = src_emb.shape[0]
    tgt_count = right_sentence_vectors.shape[0]
    own_src = lax.dynamic_slice_in_dim(src_mass, lax.axis_index(("y_hi", "x")) * src_count, src_count)
    own_tgt = lax.dynamic_slice_in_dim(
        tgt_mass, lax.axis_index(("y_lo", "z", "core")) * tgt_count, tgt_count
    )
    src_rows = split_gather(src_emb, ROWS)
    target_rows = split_gather(right_sentence_vectors, COLS)

    kernel_grid = (
        lax.dot_general(
            src_rows, target_rows, (((1,), (1,)), ((), ())), preferred_element_type=jnp.float32
        )
        / regularizer_epsilon
    )
    kernel = lax.optimization_barrier(jnp.exp(kernel_grid).astype(jnp.bfloat16))
    weighted = kernel * kernel_grid

    vector = jnp.ones((target_rows.shape[0],), jnp.float32)
    old_saved, row_saved, src_saved, col_saved, tgt_saved = ([], [], [], [], [])
    tgt_adj = None
    for iteration in range(ITERS):
        old_saved.append(vector)
        if iteration == 0:
            row_sum, src_mass = sum_and_gather(times_vector(kernel, vector), own_src, ROWS)
        else:
            row_sum = row_total(times_vector(kernel, vector))
        src_scale = src_mass / row_sum
        if iteration == ITERS - 1:
            both = col_total(
                jnp.stack([vector_times(src_scale, kernel), vector_times(src_scale, weighted)])
            )
            col_sum, tgt_adj = both[0], both[1]
        elif iteration == 0:
            col_sum, tgt_mass = sum_and_gather(vector_times(src_scale, kernel), own_tgt, COLS)
        else:
            col_sum = col_total(vector_times(src_scale, kernel))
        vector = tgt_mass / col_sum
        row_saved.append(row_sum)
        src_saved.append(src_scale)
        col_saved.append(col_sum)
        tgt_saved.append(vector)
    last_src = src_saved[-1]
    last_tgt = tgt_saved[-1]
    row_bars = [None] * ITERS
    col_bars = [None] * ITERS
    for iteration in reversed(range(ITERS)):
        col_bar = -tgt_adj * tgt_saved[iteration] / col_saved[iteration]
        part = times_vector(kernel, col_bar)
        if iteration == ITERS - 1:
            part = part + times_vector(weighted, last_tgt)
        back = row_total(part)
        row_bar = -back * src_saved[iteration] / row_saved[iteration]
        if iteration > 0:
            tgt_adj = col_total(vector_times(row_bar, kernel))
        row_bars[iteration] = row_bar
        col_bars[iteration] = col_bar
    left = jnp.stack(row_bars + src_saved, axis=1)
    right = jnp.stack(old_saved + col_bars, axis=1)
    left_pieces, right_pieces = split3(left), split3(right)
    left_all = jnp.concatenate([a for a in left_pieces for b in right_pieces], axis=1)
    right_all = jnp.concatenate([b for a in left_pieces for b in right_pieces], axis=1)
    lowrank = lax.dot_general(
        left_all, right_all, (((1,), (1,)), ((), ())), preferred_element_type=jnp.float32
    )
    cross_term_grid = (
        kernel * (last_src[:, None] * last_tgt[None, :] * (1.0 + kernel_grid) + lowrank)
    ).astype(jnp.bfloat16)
    left_share_piece = (
        jnp.dot(cross_term_grid, target_rows, preferred_element_type=jnp.float32)
        / regularizer_epsilon
    )
    right_share_piece = (
        lax.dot_general(
            cross_term_grid, src_rows, (((0,), (0,)), ((), ())), preferred_element_type=jnp.float32
        )
        / regularizer_epsilon
    )
    grad_src = split_scatter(left_share_piece, ROWS)
    grad_tgt = split_scatter(right_share_piece, COLS)
    return (grad_src, grad_tgt)


def solution(mesh):
    physical = Mesh(mesh.devices.reshape(2, 4, 2, 2, 4), PHYSICAL)
    src_axes = ("y_lo", "z", "core")
    tgt_axes = ("y_hi", "x")
    placed = (
        P(src_axes + tgt_axes, None),
        P(tgt_axes + src_axes, None),
        P(src_axes),
        P(tgt_axes),
    )
    return jax.shard_map(
        per_device,
        mesh=physical,
        in_specs=placed,
        out_specs=(P(src_axes + tgt_axes, None), P(tgt_axes + src_axes, None)),
        check_vma=False,
    )
```
